512 devices in a mesh: tok: 16 (over z), head: 32 (over y, x, core).
Axes of the slice: x: 4, y: 4, z: 16, core: 2. Of those that a mesh axis runs over, the one named last changes fastest.
Arguments:
- tokens: bfloat16 [3072, 4096], P(('tok', 'head')), may hold values from -6 to 6
- ln1_gain: float32 [4096], replicated, may hold values from 0.25 to 1.75
- ln1_bias: float32 [4096], replicated, may hold values from -1.75 to 1.75
- ln2_gain: float32 [4096], replicated, may hold values from 0.25 to 1.75
- ln2_bias: float32 [4096], replicated, may hold values from -1.75 to 1.75
- w_qkv: bfloat16 [4096, 12288], P('tok', 'head'), may hold values from -0.09375 to 0.09375
- b_qkv: float32 [12288], P('head'), may hold values from -3 to 3
- w_dense: bfloat16 [4096, 4096], P('head', 'tok'), may hold values from -0.09375 to 0.09375
- b_dense: float32 [4096], replicated, may hold values from -1.75 to 1.75
- w_up: bfloat16 [4096, 16384], P('tok', 'head'), may hold values from -0.09375 to 0.09375
- b_up: float32 [16384], P('head'), may hold values from -3 to 3
- w_down: bfloat16 [16384, 4096], P('head', 'tok'), may hold values from -0.046875 to 0.046875
- b_down: float32 [4096], replicated, may hold values from -1.75 to 1.75
- k_cache: bfloat16 [98304, 4096], P('tok', 'head'), may hold values from -610 to 610
- v_cache: bfloat16 [98304, 4096], P('tok', 'head'), may hold values from -6 to 6
- cache_lengths: int32 [16, 33], P('tok'), may hold values from 1 to 4096, 6144 in all within a row
Outputs:
- mixed: bfloat16 [3072, 4096], P(('tok', 'head'))
The draws below stay inside these ranges and needn't reach their ends.
Inputs may be any that keep to these rules, and one draw needn't show every extreme that they name: `cache_lengths`: row g lists the cache lengths of group g's 33 requests in the order in which their caches lie in the group's 6144 cache rows; every row sums to 6144. Request 0 of a group is the one whose 160 new tokens are prefilled, the others decode one token each.
All inputs are finite; a program needn't handle non-finite values.
Results may differ from the reference program's by a relative error of at most 0.02.
Values may be sent and summed in bfloat16 or wider, within the bound.
No kernel may reach another device: no remote copies, remote signals or barrier semaphores. Data moves between devices by JAX's collectives and lax.ppermute only.
A program may use at most 64 MiB of HBM per device.

```python
import math
import jax
import jax.numpy as jnp
import numpy as np
from jax import lax

D = 4096
HD = 128
ROT = 32
FF = 16384
SLOTS = 6144
CAP = 4096
WINDOW = 2048
SINKS = 4
NH = 32
GT = 192
REQ = 33
TOKENS = 3072
CACHE_ROWS = 98304
N_TOK = 16


def draw_k_cache(key, part):
    first = jax.random.fold_in(key, 0)
    width = NH * HD
    values = jax.random.truncated_normal(first, -6.0, 6.0, (CACHE_ROWS, width), jnp.float32)
    return values.astype(jnp.bfloat16)


def shard_levels(rng, shape, pieces, low, top_value):
    factor_of, own = 1.0, jax.random.fold_in(rng, 6)
    for dim, parts in pieces:
        heights = jnp.exp(jax.random.uniform(jax.random.fold_in(own, dim), (parts,), jnp.float32, low / len(pieces), top_value / len(pieces)))
        factor_of = factor_of * jnp.repeat(heights, shape[dim] // parts).reshape([-1 if axis == dim else 1 for axis in range(len(shape))])
    return factor_of


def length_profile(number_of, total, bound, slope):
    weights = [(1 << 20) // math.isqrt(grade ** slope) + 1 for grade in range(2, number_of + 1)]
    surplus, counts = total - bound - (number_of - 1), [1] * (number_of - 1)
    while surplus > 0:
        movable = [i for i in range(number_of - 1) if counts[i] < bound]
        whole, remaining = sum([weights[i] for i in movable]), surplus
        for i in movable:
            addition = min(bound - counts[i], max(1, remaining * weights[i] // whole), surplus)
            counts[i] = counts[i] + addition
            surplus = surplus - addition
    return np.array([bound] + counts)


def uneven_parts(key, number_of, total, bound, lean):
    if number_of == 2:
        one = jax.random.randint(key, (), max(1, total - bound), min(bound, total - 1) + 1)
        return jnp.stack([one, total - one])
    lengths = jnp.asarray(length_profile(number_of, total, bound, lean), jnp.int32)
    couples = (number_of - 1) // 2
    giver, receiver = lengths[1:1 + 2 * couples:2], lengths[2:2 + 2 * couples:2]
    slack = jnp.minimum(giver - 1, bound - receiver)
    moved = jax.random.randint(jax.random.fold_in(key, 1), (couples,), 0, 1 << 20) % (slack + 1)
    lengths = lengths.at[1:1 + 2 * couples:2].set(giver - moved).at[2:2 + 2 * couples:2].set(receiver + moved)
    return lengths[jax.random.permutation(jax.random.fold_in(key, 2), number_of)]


def gaussian(key, extent, scale, bound, shards=(), kind=jnp.bfloat16):
    loudness = shard_levels(key, extent, shards, -0.22, 0.18) if shards else 1.0
    entries = jax.random.normal(key, extent, jnp.float32) * scale * loudness
    return jnp.minimum(jnp.maximum(entries, -bound), bound).astype(kind)


def setup_inputs(seed: int = 0) -> dict:
    key_list = jax.random.split(jax.random.key(seed), 17)
    return {
        "tokens": gaussian(key_list[0], (TOKENS, D), 1.0, 6.0, ((0, 512),)),
        "ln1_gain": jnp.clip(1.0 + 0.15 * jax.random.normal(key_list[1], (D,), jnp.float32), 0.25, 1.75),
        "ln1_bias": gaussian(key_list[2], (D,), 0.3, 1.75, (), jnp.float32),
        "ln2_gain": jnp.clip(1.0 + 0.15 * jax.random.normal(key_list[3], (D,), jnp.float32), 0.25, 1.75),
        "ln2_bias": gaussian(key_list[4], (D,), 0.3, 1.75, (), jnp.float32),
        "w_qkv": gaussian(key_list[5], (D, NH * 3 * HD), D ** -0.5, 0.09375, ((0, 16), (1, 32))),
        "b_qkv": gaussian(key_list[6], (NH * 3 * HD,), 0.5, 3.0, ((0, 32),), jnp.float32),
        "w_dense": gaussian(key_list[7], (NH * HD, D), (NH * HD) ** -0.5, 0.09375, ((0, 32), (1, 16))),
        "b_dense": gaussian(key_list[8], (D,), 0.3, 1.75, (), jnp.float32),
        "w_up": gaussian(key_list[9], (D, FF), D ** -0.5, 0.09375, ((0, 16), (1, 32))),
        "b_up": gaussian(key_list[10], (FF,), 0.5, 3.0, ((0, 32),), jnp.float32),
        "w_down": gaussian(key_list[11], (FF, D), FF ** -0.5, 0.046875, ((0, 32), (1, 16))),
        "b_down": gaussian(key_list[12], (D,), 0.3, 1.75, (), jnp.float32),
        "k_cache": draw_k_cache(jax.random.fold_in(key_list[16], 71), 0),
        "v_cache": gaussian(key_list[14], (CACHE_ROWS, NH * HD), 1.0, 6.0, ((0, 16), (1, 32))),
        "cache_lengths": jax.vmap(lambda own: uneven_parts(own, REQ, SLOTS, CAP, 2))(jax.random.split(key_list[15], N_TOK)).reshape((N_TOK, REQ)).astype(jnp.int32),
    }


epsilon = 1e-05

def layer_norm(values, gain, shift):
    values = values.astype(jnp.float32)
    center = lax.optimization_barrier(jnp.mean(values, axis=-1, keepdims=True))
    spread = lax.optimization_barrier(jnp.mean(jnp.square(values - center), axis=-1, keepdims=True))
    return (values - center) * lax.rsqrt(spread + epsilon) * gain + shift

def rotate(values, positions):
    half = ROT // 2
    inverse = jnp.power(jnp.float32(10000.0), -jnp.arange(half, dtype=jnp.float32) * (2.0 / ROT))
    angles = positions.astype(jnp.float32).reshape(positions.shape + (1,) * (values.ndim - 1)) * inverse
    cosine = jnp.cos(angles)
    sine = jnp.sin(angles)
    first = values[..., :half]
    second = values[..., half:ROT]
    rest = values[..., ROT:]
    return jnp.concatenate([first * cosine - second * sine, second * cosine + first * sine, rest], axis=-1)

def token_layout(lengths_row, group_rows):
    requests_count = lengths_row.shape[0]
    count_pre = group_rows - (requests_count - 1)
    index = jnp.arange(group_rows, dtype=jnp.int32)
    owner = jnp.maximum(index - (count_pre - 1), 0).astype(jnp.int32)
    table = owner[:, None] == jnp.arange(requests_count, dtype=jnp.int32)[None, :]
    start = lax.optimization_barrier(jnp.sum(jnp.where(table, lengths_row[None, :], 0), axis=1)).astype(jnp.int32)
    place = (start + jnp.where(owner == 0, index, 0)).astype(jnp.int32)
    return (owner, place)

def slot_layout(lengths_row, slots):
    starts = (jnp.cumsum(lengths_row) - lengths_row).astype(jnp.int32)
    index = jnp.arange(slots, dtype=jnp.int32)
    inside = index[:, None] >= starts[None, :]
    owner = (lax.optimization_barrier(jnp.sum(inside.astype(jnp.int32), axis=1)) - 1).astype(jnp.int32)
    begin = lax.optimization_barrier(jnp.max(jnp.where(inside, starts[None, :], 0), axis=1)).astype(jnp.int32)
    return (owner, (index - begin).astype(jnp.int32))

def visible(query_owner, query_place, key_owner, key_place):
    same = query_owner[:, None] == key_owner[None, :]
    before = key_place[None, :] <= query_place[:, None]
    near = (key_place[None, :] < SINKS) | (query_place[:, None] - key_place[None, :] < WINDOW)
    return same & before & near

def reference(tokens, ln1_gain, ln1_bias, ln2_gain, ln2_bias, w_qkv, b_qkv, w_dense, b_dense, w_up, b_up, w_down, b_down, k_cache, v_cache, cache_lengths):
    scale = HD ** (-0.5)
    normed_one = layer_norm(tokens, ln1_gain, ln1_bias).astype(jnp.bfloat16)
    normed_two = layer_norm(tokens, ln2_gain, ln2_bias).astype(jnp.bfloat16)
    owners, places = jax.vmap(lambda row: token_layout(row, GT))(cache_lengths)
    flat_places = places.reshape(TOKENS)
    projected = jnp.dot(normed_one, w_qkv, preferred_element_type=jnp.float32) + b_qkv
    projected = projected.reshape(TOKENS, NH, 3, HD)
    queries = rotate(projected[:, :, 0], flat_places).astype(jnp.bfloat16)
    new_keys = rotate(projected[:, :, 1], flat_places).astype(jnp.bfloat16)
    new_values = projected[:, :, 2].astype(jnp.bfloat16)
    upward = jnp.dot(normed_two, w_up, preferred_element_type=jnp.float32) + b_up
    hidden = jax.nn.gelu(upward, approximate=False).astype(jnp.bfloat16)

    def per_group(group):
        lengths_row = lax.dynamic_index_in_dim(cache_lengths, group, 0, keepdims=False)
        query_owner, query_place = token_layout(lengths_row, GT)
        slot_owner, slot_place = slot_layout(lengths_row, SLOTS)
        key_owner = jnp.concatenate([slot_owner, query_owner])
        key_place = jnp.concatenate([slot_place, query_place])
        mask = visible(query_owner, query_place, key_owner, key_place)
        group_queries = lax.dynamic_slice_in_dim(queries, group * GT, GT, 0).transpose(1, 0, 2)
        group_keys = lax.dynamic_slice_in_dim(new_keys, group * GT, GT, 0).transpose(1, 0, 2)
        group_values = lax.dynamic_slice_in_dim(new_values, group * GT, GT, 0).transpose(1, 0, 2)
        cache_keys = lax.dynamic_slice_in_dim(k_cache, group * SLOTS, SLOTS, 0).reshape(SLOTS, NH, HD).transpose(1, 0, 2)
        cache_values = lax.dynamic_slice_in_dim(v_cache, group * SLOTS, SLOTS, 0).reshape(SLOTS, NH, HD).transpose(1, 0, 2)

        def per_head(items):
            query, cache_key, cache_value, new_key, new_value = items
            keys_all = jnp.concatenate([cache_key, new_key], axis=0)
            values_all = jnp.concatenate([cache_value, new_value], axis=0)
            scores = jnp.dot(query, keys_all.T, preferred_element_type=jnp.float32) * scale
            scores = jnp.where(mask, scores, -jnp.inf)
            top = lax.optimization_barrier(jnp.max(scores, axis=1, keepdims=True))
            weights = jnp.exp(scores - top)
            total = lax.optimization_barrier(jnp.sum(weights, axis=1, keepdims=True))
            summed = jnp.dot(weights.astype(jnp.bfloat16), values_all, preferred_element_type=jnp.float32)
            return (summed / total).astype(jnp.bfloat16)
        outputs = lax.map(per_head, (group_queries, cache_keys, cache_values, group_keys, group_values))
        return outputs.transpose(1, 0, 2).reshape(GT, NH * HD)
    attention = lax.map(per_group, jnp.arange(N_TOK, dtype=jnp.int32)).reshape(TOKENS, NH * HD)
    mixed = tokens.astype(jnp.float32) + jnp.dot(attention, w_dense, preferred_element_type=jnp.float32) + b_dense
    mixed = mixed + jnp.dot(hidden, w_down, preferred_element_type=jnp.float32) + b_down
    return mixed.astype(jnp.bfloat16)
```

```python
import jax
import jax.numpy as jnp
from jax import lax
from jax.sharding import PartitionSpec as P

HD = 128
ROT = 32
WINDOW = 2048
SINKS = 4


epsilon = 1e-05


def layer_norm(values, gain, shift):
    values = values.astype(jnp.float32)
    center = jnp.mean(values, axis=-1, keepdims=True)
    spread = jnp.mean(jnp.square(values - center), axis=-1, keepdims=True)
    return (values - center) * lax.rsqrt(spread + epsilon) * gain + shift


def rotate(values, positions):
    half = ROT // 2
    inverse = jnp.power(jnp.float32(10000.0), -jnp.arange(half, dtype=jnp.float32) * (2.0 / ROT))
    angles = (
        positions.astype(jnp.float32).reshape(positions.shape + (1,) * (values.ndim - 1)) * inverse
    )
    cosine = jnp.cos(angles)
    sine = jnp.sin(angles)
    first = values[..., :half]
    second = values[..., half:ROT]
    rest = values[..., ROT:]
    return jnp.concatenate(
        [first * cosine - second * sine, second * cosine + first * sine, rest], axis=-1
    )


def token_layout(lengths_row, group_rows):
    requests_count = lengths_row.shape[0]
    count_pre = group_rows - (requests_count - 1)
    index = jnp.arange(group_rows, dtype=jnp.int32)
    owner = jnp.maximum(index - (count_pre - 1), 0)
    table = owner[:, None] == jnp.arange(requests_count, dtype=jnp.int32)[None, :]
    start = jnp.sum(jnp.where(table, lengths_row[None, :], 0), axis=1)
    place = start + jnp.where(owner == 0, index, 0)
    return (owner, place)


def slot_layout(lengths_row, slots):
    starts = jnp.cumsum(lengths_row) - lengths_row
    index = jnp.arange(slots, dtype=jnp.int32)
    inside = index[:, None] >= starts[None, :]
    owner = jnp.sum(inside.astype(jnp.int32), axis=1) - 1
    begin = jnp.max(jnp.where(inside, starts[None, :], 0), axis=1)
    return (owner, index - begin)


def visible(query_owner, query_place, key_owner, key_place):
    same = query_owner[:, None] == key_owner[None, :]
    before = key_place[None, :] <= query_place[:, None]
    near = (key_place[None, :] < SINKS) | (query_place[:, None] - key_place[None, :] < WINDOW)
    return same & before & near


def body(
    tokens,
    ln1_gain,
    ln1_bias,
    ln2_gain,
    ln2_bias,
    w_qkv,
    b_qkv,
    w_dense,
    b_dense,
    w_up,
    b_up,
    w_down,
    b_down,
    k_cache,
    v_cache,
    cache_lengths,
):
    scale = HD ** (-0.5)
    width_qkv = w_qkv.shape[1]
    width_up = w_up.shape[1]
    width_dense = w_dense.shape[0]
    packed = jnp.concatenate([w_qkv, w_up, w_dense.T, w_down.T], axis=1)
    gathered = lax.all_gather(packed, "tok", axis=0, tiled=False)
    parts = gathered.shape[0] * gathered.shape[1]
    qkv_full = gathered[:, :, :width_qkv].reshape(parts, width_qkv)
    up_full = gathered[:, :, width_qkv : width_qkv + width_up].reshape(parts, width_up)
    offset = width_qkv + width_up
    dense_t = gathered[:, :, offset : offset + width_dense].reshape(parts, width_dense)
    down_t = gathered[:, :, offset + width_dense :].reshape(parts, -1)
    whole = lax.all_gather(tokens, "head", axis=0, tiled=True)
    normed_one = layer_norm(whole, ln1_gain, ln1_bias).astype(jnp.bfloat16)
    normed_two = layer_norm(whole, ln2_gain, ln2_bias).astype(jnp.bfloat16)
    rows_total = whole.shape[0]
    projected = jnp.dot(normed_one, qkv_full, preferred_element_type=jnp.float32) + b_qkv
    upward = jnp.dot(normed_two, up_full, preferred_element_type=jnp.float32)
    lengths_row = cache_lengths[0]
    query_owner, query_place = token_layout(lengths_row, rows_total)
    queries = rotate(projected[:, :HD], query_place).astype(jnp.bfloat16)
    new_keys = rotate(projected[:, HD : 2 * HD], query_place).astype(jnp.bfloat16)
    new_values = projected[:, 2 * HD :].astype(jnp.bfloat16)
    hidden = jax.nn.gelu(upward + b_up, approximate=False).astype(jnp.bfloat16)
    slots = k_cache.shape[0]
    slot_owner, slot_place = slot_layout(lengths_row, slots)
    cache_scores = jnp.dot(queries, k_cache.T, preferred_element_type=jnp.float32) * scale
    cache_scores = jnp.where(
        visible(query_owner, query_place, slot_owner, slot_place), cache_scores, -jnp.inf
    )
    new_scores = jnp.dot(queries, new_keys.T, preferred_element_type=jnp.float32) * scale
    new_scores = jnp.where(
        visible(query_owner, query_place, query_owner, query_place), new_scores, -jnp.inf
    )
    top = jnp.maximum(jnp.max(cache_scores, axis=1), jnp.max(new_scores, axis=1))
    cache_weights = jnp.exp(cache_scores - top[:, None])
    new_weights = jnp.exp(new_scores - top[:, None])
    total = jnp.sum(cache_weights, axis=1) + jnp.sum(new_weights, axis=1)
    summed = jnp.dot(
        cache_weights.astype(jnp.bfloat16), v_cache, preferred_element_type=jnp.float32
    ) + jnp.dot(new_weights.astype(jnp.bfloat16), new_values, preferred_element_type=jnp.float32)
    attention = (summed / total[:, None]).astype(jnp.bfloat16)
    contract = (((1,), (1,)), ((), ()))
    partial = lax.dot_general(
        attention, dense_t, contract, preferred_element_type=jnp.float32
    ) + lax.dot_general(hidden, down_t, contract, preferred_element_type=jnp.float32)
    heads = lax.axis_size("head")
    partial = partial.astype(jnp.bfloat16).reshape(heads, rows_total // heads, -1)
    partial_value = lax.psum_scatter(partial, "head", scatter_dimension=0, tiled=True)
    partial_value = partial_value.reshape(tokens.shape).astype(jnp.float32)
    mixed = tokens.astype(jnp.float32) + partial_value + b_dense + b_down
    return mixed.astype(jnp.bfloat16)


def solution(mesh):
    placed = (
        P(("tok", "head"), None),
        P(),
        P(),
        P(),
        P(),
        P("tok", "head"),
        P("head"),
        P("head", "tok"),
        P(),
        P("tok", "head"),
        P("head"),
        P("head", "tok"),
        P(),
        P("tok", "head"),
        P("tok", "head"),
        P("tok", None),
    )
    return jax.shard_map(
        body, mesh=mesh, in_specs=placed, out_specs=P(("tok", "head"), None), check_vma=False
    )
```

```python
import jax
import jax.numpy as jnp
from jax import lax
from jax.sharding import PartitionSpec as P

HD = 128
ROT = 32
WINDOW = 2048
SINKS = 4


epsilon = 1e-05


def layer_norm(values, gain, shift):
    values = values.astype(jnp.float32)
    center = jnp.mean(values, axis=-1, keepdims=True)
    spread = jnp.mean(jnp.square(values - center), axis=-1, keepdims=True)
    return (values - center) * lax.rsqrt(spread + epsilon) * gain + shift


def rotate(values, positions):
    half = ROT // 2
    inverse = jnp.power(jnp.float32(10000.0), -jnp.arange(half, dtype=jnp.float32) * (2.0 / ROT))
    angles = (
        positions.astype(jnp.float32).reshape(positions.shape + (1,) * (values.ndim - 1)) * inverse
    )
    cosine = jnp.cos(angles)
    sine = jnp.sin(angles)
    first = values[..., :half]
    second = values[..., half:ROT]
    rest = values[..., ROT:]
    return jnp.concatenate(
        [first * cosine - second * sine, second * cosine + first * sine, rest], axis=-1
    )


def token_layout(lengths_row, group_rows):
    requests_count = lengths_row.shape[0]
    count_pre = group_rows - (requests_count - 1)
    index = jnp.arange(group_rows, dtype=jnp.int32)
    owner = jnp.maximum(index - (count_pre - 1), 0)
    table = owner[:, None] == jnp.arange(requests_count, dtype=jnp.int32)[None, :]
    start = jnp.sum(jnp.where(table, lengths_row[None, :], 0), axis=1)
    place = start + jnp.where(owner == 0, index, 0)
    return (owner, place)


def slot_layout(lengths_row, slots):
    starts = jnp.cumsum(lengths_row) - lengths_row
    index = jnp.arange(slots, dtype=jnp.int32)
    inside = index[:, None] >= starts[None, :]
    owner = jnp.sum(inside.astype(jnp.int32), axis=1) - 1
    begin = jnp.max(jnp.where(inside, starts[None, :], 0), axis=1)
    return (owner, index - begin)


def visible(query_owner, query_place, key_owner, key_place):
    same = query_owner[:, None] == key_owner[None, :]
    before = key_place[None, :] <= query_place[:, None]
    near = (key_place[None, :] < SINKS) | (query_place[:, None] - key_place[None, :] < WINDOW)
    return same & before & near


def stage_pairs(size, stride, shift, total):
    pairs = []
    for index in range(total):
        sub = (index // stride) % size
        pairs.append((index, index + ((sub + shift) % size - sub) * stride))
    return pairs


def gather_stage(stacked, size, stride):
    total = lax.axis_size("head")
    sub = (lax.axis_index("head") // stride) % size
    received = [stacked] + [
        lax.ppermute(stacked, "head", stage_pairs(size, stride, shift, total))
        for shift in range(1, size)
    ]
    return jnp.take(jnp.stack(received), (sub - jnp.arange(size)) % size, axis=0)


def head_gather(block):
    by_y = gather_stage(block, 4, 8)
    by_x = gather_stage(by_y, 4, 2)
    by_core = gather_stage(by_x, 2, 1)
    ordered = by_core.transpose((2, 1, 0) + tuple(range(3, by_core.ndim)))
    return ordered.reshape((-1,) + block.shape[1:])


def scatter_stage(chunks, size, stride):
    total = lax.axis_size("head")
    sub = (lax.axis_index("head") // stride) % size
    summed = lax.dynamic_index_in_dim(chunks, sub, 0, keepdims=False)
    for shift in range(1, size):
        outgoing = lax.dynamic_index_in_dim(chunks, (sub + shift) % size, 0, keepdims=False)
        summed = summed + lax.ppermute(
            outgoing.astype(jnp.bfloat16), "head", stage_pairs(size, stride, shift, total)
        ).astype(jnp.float32)
    return summed


def head_reduce_scatter(partial, rows):
    blocks = partial.reshape((4, 4, 2, rows) + partial.shape[1:])
    by_core = scatter_stage(jnp.moveaxis(blocks, 2, 0), 2, 1)
    by_x = scatter_stage(jnp.moveaxis(by_core, 1, 0), 4, 2)
    return scatter_stage(by_x, 4, 8)


def body(
    tokens,
    ln1_gain,
    ln1_bias,
    ln2_gain,
    ln2_bias,
    w_qkv,
    b_qkv,
    w_dense,
    b_dense,
    w_up,
    b_up,
    w_down,
    b_down,
    k_cache,
    v_cache,
    cache_lengths,
):
    scale = HD ** (-0.5)
    width_qkv = w_qkv.shape[1]
    width_up = w_up.shape[1]
    width_dense = w_dense.shape[0]
    packed = jnp.concatenate([w_qkv, w_up, w_dense.T, w_down.T], axis=1)
    gathered = lax.all_gather(packed, "tok", axis=0, tiled=False)
    parts = gathered.shape[0] * gathered.shape[1]
    qkv_full = gathered[:, :, :width_qkv].reshape(parts, width_qkv)
    up_full = gathered[:, :, width_qkv : width_qkv + width_up].reshape(parts, width_up)
    offset = width_qkv + width_up
    dense_t = gathered[:, :, offset : offset + width_dense].reshape(parts, width_dense)
    down_t = gathered[:, :, offset + width_dense :].reshape(parts, -1)
    whole = head_gather(tokens)
    normed_one = layer_norm(whole, ln1_gain, ln1_bias).astype(jnp.bfloat16)
    normed_two = layer_norm(whole, ln2_gain, ln2_bias).astype(jnp.bfloat16)
    rows_total = whole.shape[0]
    projected = jnp.dot(normed_one, qkv_full, preferred_element_type=jnp.float32) + b_qkv
    upward = jnp.dot(normed_two, up_full, preferred_element_type=jnp.float32)
    lengths_row = cache_lengths[0]
    query_owner, query_place = token_layout(lengths_row, rows_total)
    queries = rotate(projected[:, :HD], query_place).astype(jnp.bfloat16)
    new_keys = rotate(projected[:, HD : 2 * HD], query_place).astype(jnp.bfloat16)
    new_values = projected[:, 2 * HD :].astype(jnp.bfloat16)
    hidden = jax.nn.gelu(upward + b_up, approximate=False).astype(jnp.bfloat16)
    slots = k_cache.shape[0]
    slot_owner, slot_place = slot_layout(lengths_row, slots)
    cache_scores = jnp.dot(queries, k_cache.T, preferred_element_type=jnp.float32) * scale
    cache_scores = jnp.where(
        visible(query_owner, query_place, slot_owner, slot_place), cache_scores, -jnp.inf
    )
    new_scores = jnp.dot(queries, new_keys.T, preferred_element_type=jnp.float32) * scale
    new_scores = jnp.where(
        visible(query_owner, query_place, query_owner, query_place), new_scores, -jnp.inf
    )
    top = jnp.maximum(jnp.max(cache_scores, axis=1), jnp.max(new_scores, axis=1))
    cache_weights = jnp.exp(cache_scores - top[:, None])
    new_weights = jnp.exp(new_scores - top[:, None])
    total = jnp.sum(cache_weights, axis=1) + jnp.sum(new_weights, axis=1)
    summed = jnp.dot(
        cache_weights.astype(jnp.bfloat16), v_cache, preferred_element_type=jnp.float32
    ) + jnp.dot(new_weights.astype(jnp.bfloat16), new_values, preferred_element_type=jnp.float32)
    attention = (summed / total[:, None]).astype(jnp.bfloat16)
    contract = (((1,), (1,)), ((), ()))
    partial = lax.dot_general(
        attention, dense_t, contract, preferred_element_type=jnp.float32
    ) + lax.dot_general(hidden, down_t, contract, preferred_element_type=jnp.float32)
    partial_value = head_reduce_scatter(partial, tokens.shape[0])
    mixed = tokens.astype(jnp.float32) + partial_value + b_dense + b_down
    return mixed.astype(jnp.bfloat16)


def solution(mesh):
    placed = (
        P(("tok", "head"), None),
        P(),
        P(),
        P(),
        P(),
        P("tok", "head"),
        P("head"),
        P("head", "tok"),
        P(),
        P("tok", "head"),
        P("head"),
        P("head", "tok"),
        P(),
        P("tok", "head"),
        P("tok", "head"),
        P("tok", None),
    )
    return jax.shard_map(
        body, mesh=mesh, in_specs=placed, out_specs=P(("tok", "head"), None), check_vma=False
    )
```

```python
import jax
import jax.numpy as jnp
from jax import lax
from jax.sharding import PartitionSpec as P

HD = 128
ROT = 32
WINDOW = 2048
SINKS = 4


epsilon = 1e-05


def layer_norm(values, gain, shift):
    values = values.astype(jnp.float32)
    center = jnp.mean(values, axis=-1, keepdims=True)
    spread = jnp.mean(jnp.square(values - center), axis=-1, keepdims=True)
    return (values - center) * lax.rsqrt(spread + epsilon) * gain + shift


def rotate(values, positions):
    half = ROT // 2
    inverse = jnp.power(jnp.float32(10000.0), -jnp.arange(half, dtype=jnp.float32) * (2.0 / ROT))
    angles = (
        positions.astype(jnp.float32).reshape(positions.shape + (1,) * (values.ndim - 1)) * inverse
    )
    cosine = jnp.cos(angles)
    sine = jnp.sin(angles)
    first = values[..., :half]
    second = values[..., half:ROT]
    rest = values[..., ROT:]
    return jnp.concatenate(
        [first * cosine - second * sine, second * cosine + first * sine, rest], axis=-1
    )


def token_layout(lengths_row, group_rows):
    requests_count = lengths_row.shape[0]
    count_pre = group_rows - (requests_count - 1)
    index = jnp.arange(group_rows, dtype=jnp.int32)
    owner = jnp.maximum(index - (count_pre - 1), 0)
    table = owner[:, None] == jnp.arange(requests_count, dtype=jnp.int32)[None, :]
    start = jnp.sum(jnp.where(table, lengths_row[None, :], 0), axis=1)
    place = start + jnp.where(owner == 0, index, 0)
    return (owner, place)


def slot_layout(lengths_row, slots):
    starts = jnp.cumsum(lengths_row) - lengths_row
    index = jnp.arange(slots, dtype=jnp.int32)
    inside = index[:, None] >= starts[None, :]
    owner = jnp.sum(inside.astype(jnp.int32), axis=1) - 1
    begin = jnp.max(jnp.where(inside, starts[None, :], 0), axis=1)
    return (owner, index - begin)


def visible(query_owner, query_place, key_owner, key_place):
    same = query_owner[:, None] == key_owner[None, :]
    before = key_place[None, :] <= query_place[:, None]
    near = (key_place[None, :] < SINKS) | (query_place[:, None] - key_place[None, :] < WINDOW)
    return same & before & near


def stage_pairs(size, stride, shift, total):
    pairs = []
    for index in range(total):
        sub = (index // stride) % size
        pairs.append((index, index + ((sub + shift) % size - sub) * stride))
    return pairs


def gather_stage(stacked, size, stride):
    total = lax.axis_size("head")
    sub = (lax.axis_index("head") // stride) % size
    received = [stacked] + [
        lax.ppermute(stacked, "head", stage_pairs(size, stride, shift, total))
        for shift in range(1, size)
    ]
    return jnp.take(jnp.stack(received), (sub - jnp.arange(size)) % size, axis=0)


def head_gather(block):
    by_y = gather_stage(block, 4, 8)
    by_x = gather_stage(by_y, 4, 2)
    by_core = gather_stage(by_x, 2, 1)
    ordered = by_core.transpose((2, 1, 0) + tuple(range(3, by_core.ndim)))
    return ordered.reshape((-1,) + block.shape[1:])


def scatter_stage(chunks, size, stride):
    total = lax.axis_size("head")
    sub = (lax.axis_index("head") // stride) % size
    summed = lax.dynamic_index_in_dim(chunks, sub, 0, keepdims=False)
    for shift in range(1, size):
        outgoing = lax.dynamic_index_in_dim(chunks, (sub + shift) % size, 0, keepdims=False)
        summed = summed + lax.ppermute(
            outgoing.astype(jnp.bfloat16), "head", stage_pairs(size, stride, shift, total)
        ).astype(jnp.float32)
    return summed


def head_reduce_scatter(partial, rows):
    blocks = partial.reshape((4, 4, 2, rows) + partial.shape[1:])
    by_core = scatter_stage(jnp.moveaxis(blocks, 2, 0), 2, 1)
    by_x = scatter_stage(jnp.moveaxis(by_core, 1, 0), 4, 2)
    return scatter_stage(by_x, 4, 8)


def body(
    tokens,
    ln1_gain,
    ln1_bias,
    ln2_gain,
    ln2_bias,
    w_qkv,
    b_qkv,
    w_dense,
    b_dense,
    w_up,
    b_up,
    w_down,
    b_down,
    k_cache,
    v_cache,
    cache_lengths,
):
    scale = HD ** (-0.5)
    width_qkv = w_qkv.shape[1]
    width_up = w_up.shape[1]
    width_dense = w_dense.shape[0]
    first = lax.all_gather(jnp.concatenate([w_qkv, w_up], axis=1), "tok", axis=0, tiled=False)
    second = lax.all_gather(
        jnp.concatenate([w_dense, w_down], axis=0), "tok", axis=0, tiled=False
    )
    parts = first.shape[0] * first.shape[1]
    qkv_full = first[:, :, :width_qkv].reshape(parts, width_qkv)
    up_full = first[:, :, width_qkv:].reshape(parts, width_up)
    dense_parts = second[:, :width_dense, :]
    down_parts = second[:, width_dense:, :]
    whole = head_gather(tokens)
    normed_one = layer_norm(whole, ln1_gain, ln1_bias).astype(jnp.bfloat16)
    normed_two = layer_norm(whole, ln2_gain, ln2_bias).astype(jnp.bfloat16)
    rows_total = whole.shape[0]
    projected = jnp.dot(normed_one, qkv_full, preferred_element_type=jnp.float32) + b_qkv
    upward = jnp.dot(normed_two, up_full, preferred_element_type=jnp.float32)
    lengths_row = cache_lengths[0]
    query_owner, query_place = token_layout(lengths_row, rows_total)
    queries = rotate(projected[:, :HD], query_place).astype(jnp.bfloat16)
    new_keys = rotate(projected[:, HD : 2 * HD], query_place).astype(jnp.bfloat16)
    new_values = projected[:, 2 * HD :].astype(jnp.bfloat16)
    hidden = jax.nn.gelu(upward + b_up, approximate=False).astype(jnp.bfloat16)
    slots = k_cache.shape[0]
    slot_owner, slot_place = slot_layout(lengths_row, slots)
    cache_scores = jnp.dot(queries, k_cache.T, preferred_element_type=jnp.float32) * scale
    cache_scores = jnp.where(
        visible(query_owner, query_place, slot_owner, slot_place), cache_scores, -jnp.inf
    )
    new_scores = jnp.dot(queries, new_keys.T, preferred_element_type=jnp.float32) * scale
    new_scores = jnp.where(
        visible(query_owner, query_place, query_owner, query_place), new_scores, -jnp.inf
    )
    top = jnp.maximum(jnp.max(cache_scores, axis=1), jnp.max(new_scores, axis=1))
    cache_weights = jnp.exp(cache_scores - top[:, None])
    new_weights = jnp.exp(new_scores - top[:, None])
    total = jnp.sum(cache_weights, axis=1) + jnp.sum(new_weights, axis=1)
    summed = jnp.dot(
        cache_weights.astype(jnp.bfloat16), v_cache, preferred_element_type=jnp.float32
    ) + jnp.dot(new_weights.astype(jnp.bfloat16), new_values, preferred_element_type=jnp.float32)
    attention = (summed / total[:, None]).astype(jnp.bfloat16)
    contract = (((1,), (1,)), ((), ()))
    partial = lax.dot_general(
        attention, dense_parts, contract, preferred_element_type=jnp.float32
    ) + lax.dot_general(hidden, down_parts, contract, preferred_element_type=jnp.float32)
    partial = partial.reshape(rows_total, -1)
    partial_value = head_reduce_scatter(partial, tokens.shape[0])
    mixed = tokens.astype(jnp.float32) + partial_value + b_dense + b_down
    return mixed.astype(jnp.bfloat16)


def solution(mesh):
    placed = (
        P(("tok", "head"), None),
        P(),
        P(),
        P(),
        P(),
        P("tok", "head"),
        P("head"),
        P("head", "tok"),
        P(),
        P("tok", "head"),
        P("head"),
        P("head", "tok"),
        P(),
        P("tok", "head"),
        P("tok", "head"),
        P("tok", None),
    )
    return jax.shard_map(
        body, mesh=mesh, in_specs=placed, out_specs=P(("tok", "head"), None), check_vma=False
    )
```

```python
import jax
import jax.numpy as jnp
from jax import lax
from jax.sharding import PartitionSpec as P

HD = 128
ROT = 32
WINDOW = 2048
SINKS = 4


epsilon = 1e-05


def layer_norm(values, gain, shift):
    values = values.astype(jnp.float32)
    center = jnp.mean(values, axis=-1, keepdims=True)
    spread = jnp.mean(jnp.square(values - center), axis=-1, keepdims=True)
    return (values - center) * lax.rsqrt(spread + epsilon) * gain + shift


def rotate(values, positions):
    half = ROT // 2
    inverse = jnp.power(jnp.float32(10000.0), -jnp.arange(half, dtype=jnp.float32) * (2.0 / ROT))
    angles = (
        positions.astype(jnp.float32).reshape(positions.shape + (1,) * (values.ndim - 1)) * inverse
    )
    cosine = jnp.cos(angles)
    sine = jnp.sin(angles)
    first = values[..., :half]
    second = values[..., half:ROT]
    rest = values[..., ROT:]
    return jnp.concatenate(
        [first * cosine - second * sine, second * cosine + first * sine, rest], axis=-1
    )


def token_layout(lengths_row, group_rows):
    requests_count = lengths_row.shape[0]
    count_pre = group_rows - (requests_count - 1)
    index = jnp.arange(group_rows, dtype=jnp.int32)
    owner = jnp.maximum(index - (count_pre - 1), 0)
    table = owner[:, None] == jnp.arange(requests_count, dtype=jnp.int32)[None, :]
    start = jnp.sum(jnp.where(table, lengths_row[None, :], 0), axis=1)
    place = start + jnp.where(owner == 0, index, 0)
    return (owner, place)


def slot_layout(lengths_row, slots):
    starts = jnp.cumsum(lengths_row) - lengths_row
    index = jnp.arange(slots, dtype=jnp.int32)
    inside = index[:, None] >= starts[None, :]
    owner = jnp.sum(inside.astype(jnp.int32), axis=1) - 1
    begin = jnp.max(jnp.where(inside, starts[None, :], 0), axis=1)
    return (owner, index - begin)


def visible(query_owner, query_place, key_owner, key_place):
    same = query_owner[:, None] == key_owner[None, :]
    before = key_place[None, :] <= query_place[:, None]
    near = (key_place[None, :] < SINKS) | (query_place[:, None] - key_place[None, :] < WINDOW)
    return same & before & near


def stage_pairs(size, stride, shift, total):
    pairs = []
    for index in range(total):
        sub = (index // stride) % size
        pairs.append((index, index + ((sub + shift) % size - sub) * stride))
    return pairs


def gather_stage(stacked, size, stride):
    total = lax.axis_size("head")
    sub = (lax.axis_index("head") // stride) % size
    received = [stacked] + [
        lax.ppermute(stacked, "head", stage_pairs(size, stride, shift, total))
        for shift in range(1, size)
    ]
    return jnp.take(jnp.stack(received), (sub - jnp.arange(size)) % size, axis=0)


def head_gather(block):
    by_y = gather_stage(block, 4, 8)
    by_x = gather_stage(by_y, 4, 2)
    by_core = gather_stage(by_x, 2, 1)
    ordered = by_core.transpose((2, 1, 0) + tuple(range(3, by_core.ndim)))
    return ordered.reshape((-1,) + block.shape[1:])


def scatter_stage(chunks, size, stride):
    total = lax.axis_size("head")
    sub = (lax.axis_index("head") // stride) % size
    summed = lax.dynamic_index_in_dim(chunks, sub, 0, keepdims=False)
    for shift in range(1, size):
        outgoing = lax.dynamic_index_in_dim(chunks, (sub + shift) % size, 0, keepdims=False)
        summed = summed + lax.ppermute(
            outgoing.astype(jnp.bfloat16), "head", stage_pairs(size, stride, shift, total)
        ).astype(jnp.float32)
    return summed


def head_reduce_scatter(partial, rows):
    blocks = partial.reshape((4, 4, 2, rows) + partial.shape[1:])
    by_core = scatter_stage(jnp.moveaxis(blocks, 2, 0), 2, 1)
    by_x = scatter_stage(jnp.moveaxis(by_core, 1, 0), 4, 2)
    return scatter_stage(by_x, 4, 8)


def body(
    tokens,
    ln1_gain,
    ln1_bias,
    ln2_gain,
    ln2_bias,
    w_qkv,
    b_qkv,
    w_dense,
    b_dense,
    w_up,
    b_up,
    w_down,
    b_down,
    k_cache,
    v_cache,
    cache_lengths,
):
    scale = HD ** (-0.5)
    width_qkv = w_qkv.shape[1]
    width_up = w_up.shape[1]
    width_dense = w_dense.shape[0]
    first = lax.all_gather(jnp.concatenate([w_qkv, w_up], axis=1), "tok", axis=0, tiled=False)
    second = lax.all_gather(
        jnp.concatenate([w_dense, w_down], axis=0), "tok", axis=0, tiled=False
    )
    parts = first.shape[0] * first.shape[1]
    qkv_full = first[:, :, :width_qkv].reshape(parts, width_qkv)
    up_full = first[:, :, width_qkv:].reshape(parts, width_up)
    dense_parts = second[:, :width_dense, :]
    down_parts = second[:, width_dense:, :]
    whole = head_gather(tokens)
    normed_one = layer_norm(whole, ln1_gain, ln1_bias).astype(jnp.bfloat16)
    normed_two = layer_norm(whole, ln2_gain, ln2_bias).astype(jnp.bfloat16)
    rows_total = whole.shape[0]
    projected = jnp.dot(normed_one, qkv_full, preferred_element_type=jnp.float32) + b_qkv
    upward = jnp.dot(normed_two, up_full, preferred_element_type=jnp.float32)
    lengths_row = cache_lengths[0]
    query_owner, query_place = token_layout(lengths_row, rows_total)
    queries = rotate(projected[:, :HD], query_place).astype(jnp.bfloat16)
    new_keys = rotate(projected[:, HD : 2 * HD], query_place).astype(jnp.bfloat16)
    new_values = projected[:, 2 * HD :].astype(jnp.bfloat16)
    hidden = jax.nn.gelu(upward + b_up, approximate=False).astype(jnp.bfloat16)
    slots = k_cache.shape[0]
    slot_owner, slot_place = slot_layout(lengths_row, slots)
    cache_scores = jnp.dot(queries, k_cache.T, preferred_element_type=jnp.float32) * scale
    cache_scores = jnp.where(
        visible(query_owner, query_place, slot_owner, slot_place), cache_scores, -jnp.inf
    )
    new_scores = jnp.dot(queries, new_keys.T, preferred_element_type=jnp.float32) * scale
    new_scores = jnp.where(
        visible(query_owner, query_place, query_owner, query_place), new_scores, -jnp.inf
    )
    top = jnp.maximum(jnp.max(cache_scores, axis=1), jnp.max(new_scores, axis=1))
    cache_weights = jnp.exp(cache_scores - top[:, None])
    new_weights = jnp.exp(new_scores - top[:, None])
    total = jnp.sum(cache_weights, axis=1) + jnp.sum(new_weights, axis=1)
    summed = jnp.dot(
        cache_weights.astype(jnp.bfloat16), v_cache, preferred_element_type=jnp.float32
    ) + jnp.dot(new_weights.astype(jnp.bfloat16), new_values, preferred_element_type=jnp.float32)
    attention = (summed / total[:, None]).astype(jnp.bfloat16)
    contract = (((1,), (1,)), ((), ()))
    partial = lax.dot_general(
        attention, dense_parts, contract, preferred_element_type=jnp.float32
    ) + lax.dot_general(hidden, down_parts, contract, preferred_element_type=jnp.float32)
    partial = partial.reshape(rows_total, -1)
    heads = lax.axis_size("head")
    blocks = partial.astype(jnp.bfloat16).reshape(heads, tokens.shape[0], -1)
    exchanged = lax.all_to_all(blocks, "head", 0, 0, tiled=True)
    partial_value = jnp.sum(exchanged.astype(jnp.float32), axis=0)
    mixed = tokens.astype(jnp.float32) + partial_value + b_dense + b_down
    return mixed.astype(jnp.bfloat16)


def solution(mesh):
    placed = (
        P(("tok", "head"), None),
        P(),
        P(),
        P(),
        P(),
        P("tok", "head"),
        P("head"),
        P("head", "tok"),
        P(),
        P("tok", "head"),
        P("head"),
        P("head", "tok"),
        P(),
        P("tok", "head"),
        P("tok", "head"),
        P("tok", None),
    )
    return jax.shard_map(
        body, mesh=mesh, in_specs=placed, out_specs=P(("tok", "head"), None), check_vma=False
    )
```

```python
import jax
import jax.numpy as jnp
from jax import lax
from jax.sharding import PartitionSpec as P

HD = 128
ROT = 32
WINDOW = 2048
SINKS = 4


epsilon = 1e-05


def layer_norm(values, gain, shift):
    values = values.astype(jnp.float32)
    center = jnp.mean(values, axis=-1, keepdims=True)
    spread = jnp.mean(jnp.square(values - center), axis=-1, keepdims=True)
    return (values - center) * lax.rsqrt(spread + epsilon) * gain + shift


def rotate(values, positions):
    half = ROT // 2
    inverse = jnp.power(jnp.float32(10000.0), -jnp.arange(half, dtype=jnp.float32) * (2.0 / ROT))
    angles = (
        positions.astype(jnp.float32).reshape(positions.shape + (1,) * (values.ndim - 1)) * inverse
    )
    cosine = jnp.cos(angles)
    sine = jnp.sin(angles)
    first = values[..., :half]
    second = values[..., half:ROT]
    rest = values[..., ROT:]
    return jnp.concatenate(
        [first * cosine - second * sine, second * cosine + first * sine, rest], axis=-1
    )


def token_layout(lengths_row, group_rows):
    requests_count = lengths_row.shape[0]
    count_pre = group_rows - (requests_count - 1)
    index = jnp.arange(group_rows, dtype=jnp.int32)
    owner = jnp.maximum(index - (count_pre - 1), 0)
    table = owner[:, None] == jnp.arange(requests_count, dtype=jnp.int32)[None, :]
    start = jnp.sum(jnp.where(table, lengths_row[None, :], 0), axis=1)
    place = start + jnp.where(owner == 0, index, 0)
    return (owner, place)


def slot_layout(lengths_row, slots):
    starts = jnp.cumsum(lengths_row) - lengths_row
    index = jnp.arange(slots, dtype=jnp.int32)
    inside = index[:, None] >= starts[None, :]
    owner = jnp.sum(inside.astype(jnp.int32), axis=1) - 1
    begin = jnp.max(jnp.where(inside, starts[None, :], 0), axis=1)
    return (owner, index - begin)


def visible(query_owner, query_place, key_owner, key_place):
    same = query_owner[:, None] == key_owner[None, :]
    before = key_place[None, :] <= query_place[:, None]
    near = (key_place[None, :] < SINKS) | (query_place[:, None] - key_place[None, :] < WINDOW)
    return same & before & near


def stage_pairs(size, stride, shift, total):
    pairs = []
    for index in range(total):
        sub = (index // stride) % size
        pairs.append((index, index + ((sub + shift) % size - sub) * stride))
    return pairs


def gather_stage(stacked, size, stride):
    total = lax.axis_size("head")
    sub = (lax.axis_index("head") // stride) % size
    received = [stacked] + [
        lax.ppermute(stacked, "head", stage_pairs(size, stride, shift, total))
        for shift in range(1, size)
    ]
    return jnp.take(jnp.stack(received), (sub - jnp.arange(size)) % size, axis=0)


def head_gather(block):
    by_y = gather_stage(block, 4, 8)
    by_x = gather_stage(by_y, 4, 2)
    by_core = gather_stage(by_x, 2, 1)
    ordered = by_core.transpose((2, 1, 0) + tuple(range(3, by_core.ndim)))
    return ordered.reshape((-1,) + block.shape[1:])


def scatter_stage(chunks, size, stride):
    total = lax.axis_size("head")
    sub = (lax.axis_index("head") // stride) % size
    summed = lax.dynamic_index_in_dim(chunks, sub, 0, keepdims=False)
    for shift in range(1, size):
        outgoing = lax.dynamic_index_in_dim(chunks, (sub + shift) % size, 0, keepdims=False)
        summed = summed + lax.ppermute(
            outgoing.astype(jnp.bfloat16), "head", stage_pairs(size, stride, shift, total)
        ).astype(jnp.float32)
    return summed


def head_reduce_scatter(partial, rows):
    blocks = partial.reshape((4, 4, 2, rows) + partial.shape[1:])
    by_core = scatter_stage(jnp.moveaxis(blocks, 2, 0), 2, 1)
    by_x = scatter_stage(jnp.moveaxis(by_core, 1, 0), 4, 2)
    return scatter_stage(by_x, 4, 8)


def body(
    tokens,
    ln1_gain,
    ln1_bias,
    ln2_gain,
    ln2_bias,
    w_qkv,
    b_qkv,
    w_dense,
    b_dense,
    w_up,
    b_up,
    w_down,
    b_down,
    k_cache,
    v_cache,
    cache_lengths,
):
    scale = HD ** (-0.5)
    width_qkv = w_qkv.shape[1]
    width_up = w_up.shape[1]
    width_dense = w_dense.shape[0]
    first = lax.all_gather(jnp.concatenate([w_qkv, w_up], axis=1), "tok", axis=0, tiled=False)
    outgoing = jnp.concatenate([w_dense, w_down], axis=0)
    half = outgoing.shape[1] // 2
    seconds = [
        lax.all_gather(outgoing[:, :half], "tok", axis=0, tiled=False),
        lax.all_gather(outgoing[:, half:], "tok", axis=0, tiled=False),
    ]
    parts = first.shape[0] * first.shape[1]
    qkv_full = first[:, :, :width_qkv].reshape(parts, width_qkv)
    up_full = first[:, :, width_qkv:].reshape(parts, width_up)
    whole = head_gather(tokens)
    normed_one = layer_norm(whole, ln1_gain, ln1_bias).astype(jnp.bfloat16)
    normed_two = layer_norm(whole, ln2_gain, ln2_bias).astype(jnp.bfloat16)
    rows_total = whole.shape[0]
    projected = jnp.dot(normed_one, qkv_full, preferred_element_type=jnp.float32) + b_qkv
    upward = jnp.dot(normed_two, up_full, preferred_element_type=jnp.float32)
    lengths_row = cache_lengths[0]
    query_owner, query_place = token_layout(lengths_row, rows_total)
    queries = rotate(projected[:, :HD], query_place).astype(jnp.bfloat16)
    new_keys = rotate(projected[:, HD : 2 * HD], query_place).astype(jnp.bfloat16)
    new_values = projected[:, 2 * HD :].astype(jnp.bfloat16)
    hidden = jax.nn.gelu(upward + b_up, approximate=False).astype(jnp.bfloat16)
    slots = k_cache.shape[0]
    slot_owner, slot_place = slot_layout(lengths_row, slots)
    cache_scores = jnp.dot(queries, k_cache.T, preferred_element_type=jnp.float32) * scale
    cache_scores = jnp.where(
        visible(query_owner, query_place, slot_owner, slot_place), cache_scores, -jnp.inf
    )
    new_scores = jnp.dot(queries, new_keys.T, preferred_element_type=jnp.float32) * scale
    new_scores = jnp.where(
        visible(query_owner, query_place, query_owner, query_place), new_scores, -jnp.inf
    )
    top = jnp.maximum(jnp.max(cache_scores, axis=1), jnp.max(new_scores, axis=1))
    cache_weights = jnp.exp(cache_scores - top[:, None])
    new_weights = jnp.exp(new_scores - top[:, None])
    total = jnp.sum(cache_weights, axis=1) + jnp.sum(new_weights, axis=1)
    summed = jnp.dot(
        cache_weights.astype(jnp.bfloat16), v_cache, preferred_element_type=jnp.float32
    ) + jnp.dot(new_weights.astype(jnp.bfloat16), new_values, preferred_element_type=jnp.float32)
    attention = (summed / total[:, None]).astype(jnp.bfloat16)
    contract = (((1,), (1,)), ((), ()))
    heads = lax.axis_size("head")
    halves = []
    for second in seconds:
        partial = lax.dot_general(
            attention, second[:, :width_dense, :], contract, preferred_element_type=jnp.float32
        ) + lax.dot_general(
            hidden, second[:, width_dense:, :], contract, preferred_element_type=jnp.float32
        )
        blocks = partial.astype(jnp.bfloat16).reshape(heads, tokens.shape[0], -1)
        exchanged = lax.all_to_all(blocks, "head", 0, 0, tiled=True)
        summed = jnp.sum(exchanged.astype(jnp.float32), axis=0)
        halves.append(summed.reshape(tokens.shape[0], -1, half))
    partial_value = jnp.concatenate(halves, axis=2).reshape(tokens.shape)
    mixed = tokens.astype(jnp.float32) + partial_value + b_dense + b_down
    return mixed.astype(jnp.bfloat16)


def solution(mesh):
    placed = (
        P(("tok", "head"), None),
        P(),
        P(),
        P(),
        P(),
        P("tok", "head"),
        P("head"),
        P("head", "tok"),
        P(),
        P("tok", "head"),
        P("head"),
        P("head", "tok"),
        P(),
        P("tok", "head"),
        P("tok", "head"),
        P("tok", None),
    )
    return jax.shard_map(
        body, mesh=mesh, in_specs=placed, out_specs=P(("tok", "head"), None), check_vma=False
    )
```

```python
import jax
import jax.numpy as jnp
from jax import lax
from jax.sharding import PartitionSpec as P

HD = 128
ROT = 32
WINDOW = 2048
SINKS = 4


epsilon = 1e-05


def layer_norm(values, gain, shift):
    values = values.astype(jnp.float32)
    center = jnp.mean(values, axis=-1, keepdims=True)
    spread = jnp.mean(jnp.square(values - center), axis=-1, keepdims=True)
    return (values - center) * lax.rsqrt(spread + epsilon) * gain + shift


def rotate(values, positions):
    half = ROT // 2
    inverse = jnp.power(jnp.float32(10000.0), -jnp.arange(half, dtype=jnp.float32) * (2.0 / ROT))
    angles = (
        positions.astype(jnp.float32).reshape(positions.shape + (1,) * (values.ndim - 1)) * inverse
    )
    cosine = jnp.cos(angles)
    sine = jnp.sin(angles)
    first = values[..., :half]
    second = values[..., half:ROT]
    rest = values[..., ROT:]
    return jnp.concatenate(
        [first * cosine - second * sine, second * cosine + first * sine, rest], axis=-1
    )


def token_layout(lengths_row, group_rows):
    requests_count = lengths_row.shape[0]
    count_pre = group_rows - (requests_count - 1)
    index = jnp.arange(group_rows, dtype=jnp.int32)
    owner = jnp.maximum(index - (count_pre - 1), 0)
    table = owner[:, None] == jnp.arange(requests_count, dtype=jnp.int32)[None, :]
    start = jnp.sum(jnp.where(table, lengths_row[None, :], 0), axis=1)
    place = start + jnp.where(owner == 0, index, 0)
    return (owner, place)


def slot_layout(lengths_row, slots):
    starts = jnp.cumsum(lengths_row) - lengths_row
    index = jnp.arange(slots, dtype=jnp.int32)
    inside = index[:, None] >= starts[None, :]
    owner = jnp.sum(inside.astype(jnp.int32), axis=1) - 1
    begin = jnp.max(jnp.where(inside, starts[None, :], 0), axis=1)
    return (owner, index - begin)


def visible(query_owner, query_place, key_owner, key_place):
    same = query_owner[:, None] == key_owner[None, :]
    before = key_place[None, :] <= query_place[:, None]
    near = (key_place[None, :] < SINKS) | (query_place[:, None] - key_place[None, :] < WINDOW)
    return same & before & near


def stage_pairs(size, stride, shift, total):
    pairs = []
    for index in range(total):
        sub = (index // stride) % size
        pairs.append((index, index + ((sub + shift) % size - sub) * stride))
    return pairs


def gather_stage(stacked, size, stride):
    total = lax.axis_size("head")
    sub = (lax.axis_index("head") // stride) % size
    received = [stacked] + [
        lax.ppermute(stacked, "head", stage_pairs(size, stride, shift, total))
        for shift in range(1, size)
    ]
    return jnp.take(jnp.stack(received), (sub - jnp.arange(size)) % size, axis=0)


def head_gather(block):
    by_y = gather_stage(block, 4, 8)
    by_x = gather_stage(by_y, 4, 2)
    by_core = gather_stage(by_x, 2, 1)
    ordered = by_core.transpose((2, 1, 0) + tuple(range(3, by_core.ndim)))
    return ordered.reshape((-1,) + block.shape[1:])


def scatter_stage(chunks, size, stride):
    total = lax.axis_size("head")
    sub = (lax.axis_index("head") // stride) % size
    summed = lax.dynamic_index_in_dim(chunks, sub, 0, keepdims=False)
    for shift in range(1, size):
        outgoing = lax.dynamic_index_in_dim(chunks, (sub + shift) % size, 0, keepdims=False)
        summed = summed + lax.ppermute(
            outgoing.astype(jnp.bfloat16), "head", stage_pairs(size, stride, shift, total)
        ).astype(jnp.float32)
    return summed


def head_reduce_scatter(partial, rows):
    blocks = partial.reshape((4, 4, 2, rows) + partial.shape[1:])
    by_core = scatter_stage(jnp.moveaxis(blocks, 2, 0), 2, 1)
    by_x = scatter_stage(jnp.moveaxis(by_core, 1, 0), 4, 2)
    return scatter_stage(by_x, 4, 8)


def tok_ring_gather(piece):
    count = lax.axis_size("tok")
    position = lax.axis_index("tok")
    forward = [(index, (index + 1) % count) for index in range(count)]
    backward = [(index, (index - 1) % count) for index in range(count)]
    by_offset = [piece] + [None] * (count - 1)
    ahead = piece
    behind = piece
    for step in range(1, count // 2 + 1):
        ahead = lax.ppermute(ahead, "tok", forward)
        by_offset[step] = ahead
        if step <= (count - 1) // 2:
            behind = lax.ppermute(behind, "tok", backward)
            by_offset[count - step] = behind
    stacked = jnp.stack(by_offset)
    return jnp.take(stacked, (position - jnp.arange(count)) % count, axis=0)


def body(
    tokens,
    ln1_gain,
    ln1_bias,
    ln2_gain,
    ln2_bias,
    w_qkv,
    b_qkv,
    w_dense,
    b_dense,
    w_up,
    b_up,
    w_down,
    b_down,
    k_cache,
    v_cache,
    cache_lengths,
):
    scale = HD ** (-0.5)
    width_qkv = w_qkv.shape[1]
    width_up = w_up.shape[1]
    width_dense = w_dense.shape[0]
    first = lax.all_gather(jnp.concatenate([w_qkv, w_up], axis=1), "tok", axis=0, tiled=False)
    second = tok_ring_gather(jnp.concatenate([w_dense, w_down], axis=0))
    parts = first.shape[0] * first.shape[1]
    qkv_full = first[:, :, :width_qkv].reshape(parts, width_qkv)
    up_full = first[:, :, width_qkv:].reshape(parts, width_up)
    dense_parts = second[:, :width_dense, :]
    down_parts = second[:, width_dense:, :]
    whole = head_gather(tokens)
    normed_one = layer_norm(whole, ln1_gain, ln1_bias).astype(jnp.bfloat16)
    normed_two = layer_norm(whole, ln2_gain, ln2_bias).astype(jnp.bfloat16)
    rows_total = whole.shape[0]
    projected = jnp.dot(normed_one, qkv_full, preferred_element_type=jnp.float32) + b_qkv
    upward = jnp.dot(normed_two, up_full, preferred_element_type=jnp.float32)
    lengths_row = cache_lengths[0]
    query_owner, query_place = token_layout(lengths_row, rows_total)
    queries = rotate(projected[:, :HD], query_place).astype(jnp.bfloat16)
    new_keys = rotate(projected[:, HD : 2 * HD], query_place).astype(jnp.bfloat16)
    new_values = projected[:, 2 * HD :].astype(jnp.bfloat16)
    hidden = jax.nn.gelu(upward + b_up, approximate=False).astype(jnp.bfloat16)
    slots = k_cache.shape[0]
    slot_owner, slot_place = slot_layout(lengths_row, slots)
    cache_scores = jnp.dot(queries, k_cache.T, preferred_element_type=jnp.float32) * scale
    cache_scores = jnp.where(
        visible(query_owner, query_place, slot_owner, slot_place), cache_scores, -jnp.inf
    )
    new_scores = jnp.dot(queries, new_keys.T, preferred_element_type=jnp.float32) * scale
    new_scores = jnp.where(
        visible(query_owner, query_place, query_owner, query_place), new_scores, -jnp.inf
    )
    top = jnp.maximum(jnp.max(cache_scores, axis=1), jnp.max(new_scores, axis=1))
    cache_weights = jnp.exp(cache_scores - top[:, None])
    new_weights = jnp.exp(new_scores - top[:, None])
    total = jnp.sum(cache_weights, axis=1) + jnp.sum(new_weights, axis=1)
    summed = jnp.dot(
        cache_weights.astype(jnp.bfloat16), v_cache, preferred_element_type=jnp.float32
    ) + jnp.dot(new_weights.astype(jnp.bfloat16), new_values, preferred_element_type=jnp.float32)
    attention = (summed / total[:, None]).astype(jnp.bfloat16)
    contract = (((1,), (1,)), ((), ()))
    partial = lax.dot_general(
        attention, dense_parts, contract, preferred_element_type=jnp.float32
    ) + lax.dot_general(hidden, down_parts, contract, preferred_element_type=jnp.float32)
    partial = partial.reshape(rows_total, -1)
    heads = lax.axis_size("head")
    blocks = partial.astype(jnp.bfloat16).reshape(heads, tokens.shape[0], -1)
    exchanged = lax.all_to_all(blocks, "head", 0, 0, tiled=True)
    partial_value = jnp.sum(exchanged.astype(jnp.float32), axis=0)
    mixed = tokens.astype(jnp.float32) + partial_value + b_dense + b_down
    return mixed.astype(jnp.bfloat16)


def solution(mesh):
    placed = (
        P(("tok", "head"), None),
        P(),
        P(),
        P(),
        P(),
        P("tok", "head"),
        P("head"),
        P("head", "tok"),
        P(),
        P("tok", "head"),
        P("head"),
        P("head", "tok"),
        P(),
        P("tok", "head"),
        P("tok", "head"),
        P("tok", None),
    )
    return jax.shard_map(
        body, mesh=mesh, in_specs=placed, out_specs=P(("tok", "head"), None), check_vma=False
    )
```

```python
import jax
import jax.numpy as jnp
from jax import lax
from jax.sharding import PartitionSpec as P

HD = 128
ROT = 32
WINDOW = 2048
SINKS = 4


epsilon = 1e-05


def layer_norm(values, gain, shift):
    values = values.astype(jnp.float32)
    center = jnp.mean(values, axis=-1, keepdims=True)
    spread = jnp.mean(jnp.square(values - center), axis=-1, keepdims=True)
    return (values - center) * lax.rsqrt(spread + epsilon) * gain + shift


def rotate(values, positions):
    half = ROT // 2
    inverse = jnp.power(jnp.float32(10000.0), -jnp.arange(half, dtype=jnp.float32) * (2.0 / ROT))
    angles = (
        positions.astype(jnp.float32).reshape(positions.shape + (1,) * (values.ndim - 1)) * inverse
    )
    cosine = jnp.cos(angles)
    sine = jnp.sin(angles)
    first = values[..., :half]
    second = values[..., half:ROT]
    rest = values[..., ROT:]
    return jnp.concatenate(
        [first * cosine - second * sine, second * cosine + first * sine, rest], axis=-1
    )


def token_layout(lengths_row, group_rows):
    requests_count = lengths_row.shape[0]
    count_pre = group_rows - (requests_count - 1)
    index = jnp.arange(group_rows, dtype=jnp.int32)
    owner = jnp.maximum(index - (count_pre - 1), 0)
    table = owner[:, None] == jnp.arange(requests_count, dtype=jnp.int32)[None, :]
    start = jnp.sum(jnp.where(table, lengths_row[None, :], 0), axis=1)
    place = start + jnp.where(owner == 0, index, 0)
    return (owner, place)


def slot_layout(lengths_row, slots):
    starts = jnp.cumsum(lengths_row) - lengths_row
    index = jnp.arange(slots, dtype=jnp.int32)
    inside = index[:, None] >= starts[None, :]
    owner = jnp.sum(inside.astype(jnp.int32), axis=1) - 1
    begin = jnp.max(jnp.where(inside, starts[None, :], 0), axis=1)
    return (owner, index - begin)


def visible(query_owner, query_place, key_owner, key_place):
    same = query_owner[:, None] == key_owner[None, :]
    before = key_place[None, :] <= query_place[:, None]
    near = (key_place[None, :] < SINKS) | (query_place[:, None] - key_place[None, :] < WINDOW)
    return same & before & near


def stage_pairs(size, stride, shift, total):
    pairs = []
    for index in range(total):
        sub = (index // stride) % size
        pairs.append((index, index + ((sub + shift) % size - sub) * stride))
    return pairs


def gather_stage(stacked, size, stride):
    total = lax.axis_size("head")
    sub = (lax.axis_index("head") // stride) % size
    received = [stacked] + [
        lax.ppermute(stacked, "head", stage_pairs(size, stride, shift, total))
        for shift in range(1, size)
    ]
    return jnp.take(jnp.stack(received), (sub - jnp.arange(size)) % size, axis=0)


def head_gather(block):
    by_y = gather_stage(block, 4, 8)
    by_x = gather_stage(by_y, 4, 2)
    by_core = gather_stage(by_x, 2, 1)
    ordered = by_core.transpose((2, 1, 0) + tuple(range(3, by_core.ndim)))
    return ordered.reshape((-1,) + block.shape[1:])


def scatter_stage(chunks, size, stride):
    total = lax.axis_size("head")
    sub = (lax.axis_index("head") // stride) % size
    summed = lax.dynamic_index_in_dim(chunks, sub, 0, keepdims=False)
    for shift in range(1, size):
        outgoing = lax.dynamic_index_in_dim(chunks, (sub + shift) % size, 0, keepdims=False)
        summed = summed + lax.ppermute(
            outgoing.astype(jnp.bfloat16), "head", stage_pairs(size, stride, shift, total)
        ).astype(jnp.float32)
    return summed


def head_reduce_scatter(partial, rows):
    blocks = partial.reshape((4, 4, 2, rows) + partial.shape[1:])
    by_core = scatter_stage(jnp.moveaxis(blocks, 2, 0), 2, 1)
    by_x = scatter_stage(jnp.moveaxis(by_core, 1, 0), 4, 2)
    return scatter_stage(by_x, 4, 8)


def body(
    tokens,
    ln1_gain,
    ln1_bias,
    ln2_gain,
    ln2_bias,
    w_qkv,
    b_qkv,
    w_dense,
    b_dense,
    w_up,
    b_up,
    w_down,
    b_down,
    k_cache,
    v_cache,
    cache_lengths,
):
    scale = HD ** (-0.5)
    width_qkv = w_qkv.shape[1]
    width_up = w_up.shape[1]
    width_dense = w_dense.shape[0]
    first = lax.all_gather(jnp.concatenate([w_qkv, w_up], axis=1), "tok", axis=0, tiled=False)
    second = lax.all_gather(
        jnp.concatenate([w_dense, w_down], axis=0), "tok", axis=0, tiled=False
    )
    parts = first.shape[0] * first.shape[1]
    qkv_full = first[:, :, :width_qkv].reshape(parts, width_qkv)
    up_full = first[:, :, width_qkv:].reshape(parts, width_up)
    dense_parts = second[:, :width_dense, :]
    down_parts = second[:, width_dense:, :]
    whole = head_gather(tokens)
    normed_one = layer_norm(whole, ln1_gain, ln1_bias).astype(jnp.bfloat16)
    normed_two = layer_norm(whole, ln2_gain, ln2_bias).astype(jnp.bfloat16)
    rows_total = whole.shape[0]
    projected = jnp.dot(normed_one, qkv_full, preferred_element_type=jnp.float32) + b_qkv
    upward = jnp.dot(normed_two, up_full, preferred_element_type=jnp.float32)
    lengths_row = cache_lengths[0]
    query_owner, query_place = token_layout(lengths_row, rows_total)
    queries = rotate(projected[:, :HD], query_place).astype(jnp.bfloat16)
    new_keys = rotate(projected[:, HD : 2 * HD], query_place).astype(jnp.bfloat16)
    new_values = projected[:, 2 * HD :].astype(jnp.bfloat16)
    hidden = jax.nn.gelu(upward + b_up, approximate=False).astype(jnp.bfloat16)
    slots = k_cache.shape[0]
    slot_owner, slot_place = slot_layout(lengths_row, slots)
    cache_scores = jnp.dot(queries, k_cache.T, preferred_element_type=jnp.float32) * scale
    cache_scores = jnp.where(
        visible(query_owner, query_place, slot_owner, slot_place), cache_scores, -jnp.inf
    )
    new_scores = jnp.dot(queries, new_keys.T, preferred_element_type=jnp.float32) * scale
    new_scores = jnp.where(
        visible(query_owner, query_place, query_owner, query_place), new_scores, -jnp.inf
    )
    top = jnp.maximum(jnp.max(cache_scores, axis=1), jnp.max(new_scores, axis=1))
    cache_weights = jnp.exp(cache_scores - top[:, None])
    new_weights = jnp.exp(new_scores - top[:, None])
    total = jnp.sum(cache_weights, axis=1) + jnp.sum(new_weights, axis=1)
    summed = jnp.dot(
        cache_weights.astype(jnp.bfloat16), v_cache, preferred_element_type=jnp.float32
    ) + jnp.dot(new_weights.astype(jnp.bfloat16), new_values, preferred_element_type=jnp.float32)
    attention = (summed / total[:, None]).astype(jnp.bfloat16)
    contract = (((1,), (1,)), ((), ()))
    partial = lax.dot_general(
        attention, dense_parts, contract, preferred_element_type=jnp.float32
    ) + lax.dot_general(hidden, down_parts, contract, preferred_element_type=jnp.float32)
    partial = partial.reshape(rows_total, -1)
    heads = lax.axis_size("head")
    blocks = partial.reshape(heads // 2, 2, tokens.shape[0], -1)
    core = lax.axis_index("head") % 2
    mine = lax.dynamic_index_in_dim(blocks, core, 1, keepdims=False)
    theirs = lax.dynamic_index_in_dim(blocks, 1 - core, 1, keepdims=False)
    swapped = lax.ppermute(
        theirs.astype(jnp.bfloat16), "head", [(index, index ^ 1) for index in range(heads)]
    )
    chip_sum = (mine + swapped.astype(jnp.float32)).astype(jnp.bfloat16)
    groups = [list(range(side, heads, 2)) for side in range(2)]
    exchanged = lax.all_to_all(chip_sum, "head", 0, 0, axis_index_groups=groups, tiled=True)
    partial_value = jnp.sum(exchanged.astype(jnp.float32), axis=0)
    mixed = tokens.astype(jnp.float32) + partial_value + b_dense + b_down
    return mixed.astype(jnp.bfloat16)


def solution(mesh):
    placed = (
        P(("tok", "head"), None),
        P(),
        P(),
        P(),
        P(),
        P("tok", "head"),
        P("head"),
        P("head", "tok"),
        P(),
        P("tok", "head"),
        P("head"),
        P("head", "tok"),
        P(),
        P("tok", "head"),
        P("tok", "head"),
        P("tok", None),
    )
    return jax.shard_map(
        body, mesh=mesh, in_specs=placed, out_specs=P(("tok", "head"), None), check_vma=False
    )
```

```python
import jax
import jax.numpy as jnp
from jax import lax
from jax.sharding import PartitionSpec as P

HD = 128
ROT = 32
WINDOW = 2048
SINKS = 4


epsilon = 1e-05


def layer_norm(values, gain, shift):
    values = values.astype(jnp.float32)
    center = jnp.mean(values, axis=-1, keepdims=True)
    spread = jnp.mean(jnp.square(values - center), axis=-1, keepdims=True)
    return (values - center) * lax.rsqrt(spread + epsilon) * gain + shift


def rotate(values, positions):
    half = ROT // 2
    inverse = jnp.power(jnp.float32(10000.0), -jnp.arange(half, dtype=jnp.float32) * (2.0 / ROT))
    angles = (
        positions.astype(jnp.float32).reshape(positions.shape + (1,) * (values.ndim - 1)) * inverse
    )
    cosine = jnp.cos(angles)
    sine = jnp.sin(angles)
    first = values[..., :half]
    second = values[..., half:ROT]
    rest = values[..., ROT:]
    return jnp.concatenate(
        [first * cosine - second * sine, second * cosine + first * sine, rest], axis=-1
    )


def token_layout(lengths_row, group_rows):
    requests_count = lengths_row.shape[0]
    count_pre = group_rows - (requests_count - 1)
    index = jnp.arange(group_rows, dtype=jnp.int32)
    owner = jnp.maximum(index - (count_pre - 1), 0)
    table = owner[:, None] == jnp.arange(requests_count, dtype=jnp.int32)[None, :]
    start = jnp.sum(jnp.where(table, lengths_row[None, :], 0), axis=1)
    place = start + jnp.where(owner == 0, index, 0)
    return (owner, place)


def slot_layout(lengths_row, slots):
    starts = jnp.cumsum(lengths_row) - lengths_row
    index = jnp.arange(slots, dtype=jnp.int32)
    inside = index[:, None] >= starts[None, :]
    owner = jnp.sum(inside.astype(jnp.int32), axis=1) - 1
    begin = jnp.max(jnp.where(inside, starts[None, :], 0), axis=1)
    return (owner, index - begin)


def visible(query_owner, query_place, key_owner, key_place):
    same = query_owner[:, None] == key_owner[None, :]
    before = key_place[None, :] <= query_place[:, None]
    near = (key_place[None, :] < SINKS) | (query_place[:, None] - key_place[None, :] < WINDOW)
    return same & before & near


def stage_pairs(size, stride, shift, total):
    pairs = []
    for index in range(total):
        sub = (index // stride) % size
        pairs.append((index, index + ((sub + shift) % size - sub) * stride))
    return pairs


def gather_stage(stacked, size, stride):
    total = lax.axis_size("head")
    sub = (lax.axis_index("head") // stride) % size
    received = [stacked] + [
        lax.ppermute(stacked, "head", stage_pairs(size, stride, shift, total))
        for shift in range(1, size)
    ]
    return jnp.take(jnp.stack(received), (sub - jnp.arange(size)) % size, axis=0)


def head_gather(block):
    by_y = gather_stage(block, 4, 8)
    by_x = gather_stage(by_y, 4, 2)
    by_core = gather_stage(by_x, 2, 1)
    ordered = by_core.transpose((2, 1, 0) + tuple(range(3, by_core.ndim)))
    return ordered.reshape((-1,) + block.shape[1:])


def scatter_stage(chunks, size, stride):
    total = lax.axis_size("head")
    sub = (lax.axis_index("head") // stride) % size
    summed = lax.dynamic_index_in_dim(chunks, sub, 0, keepdims=False)
    for shift in range(1, size):
        outgoing = lax.dynamic_index_in_dim(chunks, (sub + shift) % size, 0, keepdims=False)
        summed = summed + lax.ppermute(
            outgoing.astype(jnp.bfloat16), "head", stage_pairs(size, stride, shift, total)
        ).astype(jnp.float32)
    return summed


def head_reduce_scatter(partial, rows):
    blocks = partial.reshape((4, 4, 2, rows) + partial.shape[1:])
    by_core = scatter_stage(jnp.moveaxis(blocks, 2, 0), 2, 1)
    by_x = scatter_stage(jnp.moveaxis(by_core, 1, 0), 4, 2)
    return scatter_stage(by_x, 4, 8)


def body(
    tokens,
    ln1_gain,
    ln1_bias,
    ln2_gain,
    ln2_bias,
    w_qkv,
    b_qkv,
    w_dense,
    b_dense,
    w_up,
    b_up,
    w_down,
    b_down,
    k_cache,
    v_cache,
    cache_lengths,
):
    scale = HD ** (-0.5)
    width_qkv = w_qkv.shape[1]
    width_up = w_up.shape[1]
    width_dense = w_dense.shape[0]
    first = lax.all_gather(jnp.concatenate([w_qkv, w_up], axis=1), "tok", axis=0, tiled=False)
    second = lax.all_gather(
        jnp.concatenate([w_dense, w_down], axis=0), "tok", axis=1, tiled=True
    )
    parts = first.shape[0] * first.shape[1]
    qkv_full = first[:, :, :width_qkv].reshape(parts, width_qkv)
    up_full = first[:, :, width_qkv:].reshape(parts, width_up)
    dense_full = second[:width_dense]
    down_full = second[width_dense:]
    whole = head_gather(tokens)
    normed_one = layer_norm(whole, ln1_gain, ln1_bias).astype(jnp.bfloat16)
    normed_two = layer_norm(whole, ln2_gain, ln2_bias).astype(jnp.bfloat16)
    rows_total = whole.shape[0]
    projected = jnp.dot(normed_one, qkv_full, preferred_element_type=jnp.float32) + b_qkv
    upward = jnp.dot(normed_two, up_full, preferred_element_type=jnp.float32)
    lengths_row = cache_lengths[0]
    query_owner, query_place = token_layout(lengths_row, rows_total)
    queries = rotate(projected[:, :HD], query_place).astype(jnp.bfloat16)
    new_keys = rotate(projected[:, HD : 2 * HD], query_place).astype(jnp.bfloat16)
    new_values = projected[:, 2 * HD :].astype(jnp.bfloat16)
    hidden = jax.nn.gelu(upward + b_up, approximate=False).astype(jnp.bfloat16)
    slots = k_cache.shape[0]
    slot_owner, slot_place = slot_layout(lengths_row, slots)
    cache_scores = jnp.dot(queries, k_cache.T, preferred_element_type=jnp.float32) * scale
    cache_scores = jnp.where(
        visible(query_owner, query_place, slot_owner, slot_place), cache_scores, -jnp.inf
    )
    new_scores = jnp.dot(queries, new_keys.T, preferred_element_type=jnp.float32) * scale
    new_scores = jnp.where(
        visible(query_owner, query_place, query_owner, query_place), new_scores, -jnp.inf
    )
    top = jnp.maximum(jnp.max(cache_scores, axis=1), jnp.max(new_scores, axis=1))
    cache_weights = jnp.exp(cache_scores - top[:, None])
    new_weights = jnp.exp(new_scores - top[:, None])
    total = jnp.sum(cache_weights, axis=1) + jnp.sum(new_weights, axis=1)
    summed = jnp.dot(
        cache_weights.astype(jnp.bfloat16), v_cache, preferred_element_type=jnp.float32
    ) + jnp.dot(new_weights.astype(jnp.bfloat16), new_values, preferred_element_type=jnp.float32)
    attention = (summed / total[:, None]).astype(jnp.bfloat16)
    partial = jnp.dot(attention, dense_full, preferred_element_type=jnp.float32) + jnp.dot(
        hidden, down_full, preferred_element_type=jnp.float32
    )
    heads = lax.axis_size("head")
    blocks = partial.astype(jnp.bfloat16).reshape(heads, tokens.shape[0], -1)
    exchanged = lax.all_to_all(blocks, "head", 0, 0, tiled=True)
    partial_value = jnp.sum(exchanged.astype(jnp.float32), axis=0)
    mixed = tokens.astype(jnp.float32) + partial_value + b_dense + b_down
    return mixed.astype(jnp.bfloat16)


def solution(mesh):
    placed = (
        P(("tok", "head"), None),
        P(),
        P(),
        P(),
        P(),
        P("tok", "head"),
        P("head"),
        P("head", "tok"),
        P(),
        P("tok", "head"),
        P("head"),
        P("head", "tok"),
        P(),
        P("tok", "head"),
        P("tok", "head"),
        P("tok", None),
    )
    return jax.shard_map(
        body, mesh=mesh, in_specs=placed, out_specs=P(("tok", "head"), None), check_vma=False
    )
```

```python
import jax
import jax.numpy as jnp
from jax import lax
from jax.sharding import PartitionSpec as P

HD = 128
ROT = 32
WINDOW = 2048
SINKS = 4


epsilon = 1e-05


def layer_norm(values, gain, shift):
    values = values.astype(jnp.float32)
    center = jnp.mean(values, axis=-1, keepdims=True)
    spread = jnp.mean(jnp.square(values - center), axis=-1, keepdims=True)
    return (values - center) * lax.rsqrt(spread + epsilon) * gain + shift


def rotate(values, positions):
    half = ROT // 2
    inverse = jnp.power(jnp.float32(10000.0), -jnp.arange(half, dtype=jnp.float32) * (2.0 / ROT))
    angles = (
        positions.astype(jnp.float32).reshape(positions.shape + (1,) * (values.ndim - 1)) * inverse
    )
    cosine = jnp.cos(angles)
    sine = jnp.sin(angles)
    first = values[..., :half]
    second = values[..., half:ROT]
    rest = values[..., ROT:]
    return jnp.concatenate(
        [first * cosine - second * sine, second * cosine + first * sine, rest], axis=-1
    )


def token_layout(lengths_row, group_rows):
    requests_count = lengths_row.shape[0]
    count_pre = group_rows - (requests_count - 1)
    index = jnp.arange(group_rows, dtype=jnp.int32)
    owner = jnp.maximum(index - (count_pre - 1), 0)
    table = owner[:, None] == jnp.arange(requests_count, dtype=jnp.int32)[None, :]
    start = jnp.sum(jnp.where(table, lengths_row[None, :], 0), axis=1)
    place = start + jnp.where(owner == 0, index, 0)
    return (owner, place)


def slot_layout(lengths_row, slots):
    starts = jnp.cumsum(lengths_row) - lengths_row
    index = jnp.arange(slots, dtype=jnp.int32)
    inside = index[:, None] >= starts[None, :]
    owner = jnp.sum(inside.astype(jnp.int32), axis=1) - 1
    begin = jnp.max(jnp.where(inside, starts[None, :], 0), axis=1)
    return (owner, index - begin)


def visible(query_owner, query_place, key_owner, key_place):
    same = query_owner[:, None] == key_owner[None, :]
    before = key_place[None, :] <= query_place[:, None]
    near = (key_place[None, :] < SINKS) | (query_place[:, None] - key_place[None, :] < WINDOW)
    return same & before & near


def stage_pairs(size, stride, shift, total):
    pairs = []
    for index in range(total):
        sub = (index // stride) % size
        pairs.append((index, index + ((sub + shift) % size - sub) * stride))
    return pairs


def gather_stage(stacked, size, stride):
    total = lax.axis_size("head")
    sub = (lax.axis_index("head") // stride) % size
    received = [stacked] + [
        lax.ppermute(stacked, "head", stage_pairs(size, stride, shift, total))
        for shift in range(1, size)
    ]
    return jnp.take(jnp.stack(received), (sub - jnp.arange(size)) % size, axis=0)


def head_gather(block):
    by_y = gather_stage(block, 4, 8)
    by_x = gather_stage(by_y, 4, 2)
    by_core = gather_stage(by_x, 2, 1)
    ordered = by_core.transpose((2, 1, 0) + tuple(range(3, by_core.ndim)))
    return ordered.reshape((-1,) + block.shape[1:])


def scatter_stage(chunks, size, stride):
    total = lax.axis_size("head")
    sub = (lax.axis_index("head") // stride) % size
    summed = lax.dynamic_index_in_dim(chunks, sub, 0, keepdims=False)
    for shift in range(1, size):
        outgoing = lax.dynamic_index_in_dim(chunks, (sub + shift) % size, 0, keepdims=False)
        summed = summed + lax.ppermute(
            outgoing.astype(jnp.bfloat16), "head", stage_pairs(size, stride, shift, total)
        ).astype(jnp.float32)
    return summed


def head_reduce_scatter(partial, rows):
    blocks = partial.reshape((4, 4, 2, rows) + partial.shape[1:])
    by_core = scatter_stage(jnp.moveaxis(blocks, 2, 0), 2, 1)
    by_x = scatter_stage(jnp.moveaxis(by_core, 1, 0), 4, 2)
    return scatter_stage(by_x, 4, 8)


def body(
    tokens,
    ln1_gain,
    ln1_bias,
    ln2_gain,
    ln2_bias,
    w_qkv,
    b_qkv,
    w_dense,
    b_dense,
    w_up,
    b_up,
    w_down,
    b_down,
    k_cache,
    v_cache,
    cache_lengths,
):
    scale = HD ** (-0.5)
    width_qkv = w_qkv.shape[1]
    width_up = w_up.shape[1]
    first = lax.all_gather(jnp.concatenate([w_qkv, w_up], axis=1), "tok", axis=0, tiled=False)
    second = lax.all_gather(
        jnp.concatenate([w_dense, w_down], axis=0), "tok", axis=0, tiled=False
    )
    parts = first.shape[0] * first.shape[1]
    qkv_full = first[:, :, :width_qkv].reshape(parts, width_qkv)
    up_full = first[:, :, width_qkv:].reshape(parts, width_up)
    whole = head_gather(tokens)
    normed_one = layer_norm(whole, ln1_gain, ln1_bias).astype(jnp.bfloat16)
    normed_two = layer_norm(whole, ln2_gain, ln2_bias).astype(jnp.bfloat16)
    rows_total = whole.shape[0]
    projected = jnp.dot(normed_one, qkv_full, preferred_element_type=jnp.float32) + b_qkv
    upward = jnp.dot(normed_two, up_full, preferred_element_type=jnp.float32)
    lengths_row = cache_lengths[0]
    query_owner, query_place = token_layout(lengths_row, rows_total)
    queries = rotate(projected[:, :HD], query_place).astype(jnp.bfloat16)
    new_keys = rotate(projected[:, HD : 2 * HD], query_place).astype(jnp.bfloat16)
    new_values = projected[:, 2 * HD :].astype(jnp.bfloat16)
    hidden = jax.nn.gelu(upward + b_up, approximate=False).astype(jnp.bfloat16)
    slots = k_cache.shape[0]
    slot_owner, slot_place = slot_layout(lengths_row, slots)
    cache_scores = jnp.dot(queries, k_cache.T, preferred_element_type=jnp.float32) * scale
    cache_scores = jnp.where(
        visible(query_owner, query_place, slot_owner, slot_place), cache_scores, -jnp.inf
    )
    new_scores = jnp.dot(queries, new_keys.T, preferred_element_type=jnp.float32) * scale
    new_scores = jnp.where(
        visible(query_owner, query_place, query_owner, query_place), new_scores, -jnp.inf
    )
    top = jnp.maximum(jnp.max(cache_scores, axis=1), jnp.max(new_scores, axis=1))
    cache_weights = jnp.exp(cache_scores - top[:, None])
    new_weights = jnp.exp(new_scores - top[:, None])
    total = jnp.sum(cache_weights, axis=1) + jnp.sum(new_weights, axis=1)
    summed = jnp.dot(
        cache_weights.astype(jnp.bfloat16), v_cache, preferred_element_type=jnp.float32
    ) + jnp.dot(new_weights.astype(jnp.bfloat16), new_values, preferred_element_type=jnp.float32)
    attention = (summed / total[:, None]).astype(jnp.bfloat16)
    contract = (((1,), (1,)), ((), ()))
    mixed_in = jnp.concatenate([attention, hidden], axis=1)
    partial = lax.dot_general(mixed_in, second, contract, preferred_element_type=jnp.float32)
    partial = partial.reshape(rows_total, -1)
    heads = lax.axis_size("head")
    blocks = partial.astype(jnp.bfloat16).reshape(heads, tokens.shape[0], -1)
    exchanged = lax.all_to_all(blocks, "head", 0, 0, tiled=True)
    partial_value = jnp.sum(exchanged.astype(jnp.float32), axis=0)
    mixed = tokens.astype(jnp.float32) + partial_value + b_dense + b_down
    return mixed.astype(jnp.bfloat16)


def solution(mesh):
    placed = (
        P(("tok", "head"), None),
        P(),
        P(),
        P(),
        P(),
        P("tok", "head"),
        P("head"),
        P("head", "tok"),
        P(),
        P("tok", "head"),
        P("head"),
        P("head", "tok"),
        P(),
        P("tok", "head"),
        P("tok", "head"),
        P("tok", None),
    )
    return jax.shard_map(
        body, mesh=mesh, in_specs=placed, out_specs=P(("tok", "head"), None), check_vma=False
    )
```

```python
import jax
import numpy as np
import jax.numpy as jnp
from jax import lax
from jax.sharding import PartitionSpec as P

HD = 128
ROT = 32
WINDOW = 2048
SINKS = 4


epsilon = 1e-05


def layer_norm(values, gain, shift):
    values = values.astype(jnp.float32)
    center = jnp.mean(values, axis=-1, keepdims=True)
    spread = jnp.mean(jnp.square(values - center), axis=-1, keepdims=True)
    return (values - center) * lax.rsqrt(spread + epsilon) * gain + shift


def rotate(values, positions):
    half = ROT // 2
    inverse = jnp.power(jnp.float32(10000.0), -jnp.arange(half, dtype=jnp.float32) * (2.0 / ROT))
    angles = (
        positions.astype(jnp.float32).reshape(positions.shape + (1,) * (values.ndim - 1)) * inverse
    )
    cosine = jnp.cos(angles)
    sine = jnp.sin(angles)
    first = values[..., :half]
    second = values[..., half:ROT]
    rest = values[..., ROT:]
    return jnp.concatenate(
        [first * cosine - second * sine, second * cosine + first * sine, rest], axis=-1
    )


def token_layout(lengths_row, group_rows):
    requests_count = lengths_row.shape[0]
    count_pre = group_rows - (requests_count - 1)
    index = jnp.arange(group_rows, dtype=jnp.int32)
    owner = jnp.maximum(index - (count_pre - 1), 0)
    table = owner[:, None] == jnp.arange(requests_count, dtype=jnp.int32)[None, :]
    start = jnp.sum(jnp.where(table, lengths_row[None, :], 0), axis=1)
    place = start + jnp.where(owner == 0, index, 0)
    return (owner, place)


def slot_layout(lengths_row, slots):
    starts = jnp.cumsum(lengths_row) - lengths_row
    index = jnp.arange(slots, dtype=jnp.int32)
    inside = index[:, None] >= starts[None, :]
    owner = jnp.sum(inside.astype(jnp.int32), axis=1) - 1
    begin = jnp.max(jnp.where(inside, starts[None, :], 0), axis=1)
    return (owner, index - begin)


def visible(query_owner, query_place, key_owner, key_place):
    same = query_owner[:, None] == key_owner[None, :]
    before = key_place[None, :] <= query_place[:, None]
    near = (key_place[None, :] < SINKS) | (query_place[:, None] - key_place[None, :] < WINDOW)
    return same & before & near


def stage_pairs(size, stride, shift, total):
    pairs = []
    for index in range(total):
        sub = (index // stride) % size
        pairs.append((index, index + ((sub + shift) % size - sub) * stride))
    return pairs


def gather_stage(stacked, size, stride):
    total = lax.axis_size("head")
    sub = (lax.axis_index("head") // stride) % size
    received = [stacked] + [
        lax.ppermute(stacked, "head", stage_pairs(size, stride, shift, total))
        for shift in range(1, size)
    ]
    return jnp.take(jnp.stack(received), (sub - jnp.arange(size)) % size, axis=0)


def head_gather(block):
    by_y = gather_stage(block, 4, 8)
    by_x = gather_stage(by_y, 4, 2)
    by_core = gather_stage(by_x, 2, 1)
    ordered = by_core.transpose((0, 2, 1) + tuple(range(3, by_core.ndim)))
    return ordered.reshape((-1,) + block.shape[1:])


def scatter_stage(chunks, size, stride):
    total = lax.axis_size("head")
    sub = (lax.axis_index("head") // stride) % size
    summed = lax.dynamic_index_in_dim(chunks, sub, 0, keepdims=False)
    for shift in range(1, size):
        outgoing = lax.dynamic_index_in_dim(chunks, (sub + shift) % size, 0, keepdims=False)
        summed = summed + lax.ppermute(
            outgoing.astype(jnp.bfloat16), "head", stage_pairs(size, stride, shift, total)
        ).astype(jnp.float32)
    return summed


def head_reduce_scatter(partial, rows):
    blocks = partial.reshape((4, 4, 2, rows) + partial.shape[1:])
    by_core = scatter_stage(jnp.moveaxis(blocks, 2, 0), 2, 1)
    by_x = scatter_stage(jnp.moveaxis(by_core, 1, 0), 4, 2)
    return scatter_stage(by_x, 4, 8)


def body(
    tokens,
    ln1_gain,
    ln1_bias,
    ln2_gain,
    ln2_bias,
    w_qkv,
    b_qkv,
    w_dense,
    b_dense,
    w_up,
    b_up,
    w_down,
    b_down,
    k_cache,
    v_cache,
    cache_lengths,
):
    scale = HD ** (-0.5)
    width_qkv = w_qkv.shape[1]
    width_up = w_up.shape[1]
    first = lax.all_gather(jnp.concatenate([w_qkv, w_up], axis=1), "tok", axis=0, tiled=False)
    second = lax.all_gather(
        jnp.concatenate([w_dense, w_down], axis=0), "tok", axis=0, tiled=False
    )
    parts = first.shape[0] * first.shape[1]
    qkv_full = first[:, :, :width_qkv].reshape(parts, width_qkv)
    up_full = first[:, :, width_qkv:].reshape(parts, width_up)
    whole = head_gather(tokens)
    normed_one = layer_norm(whole, ln1_gain, ln1_bias).astype(jnp.bfloat16)
    normed_two = layer_norm(whole, ln2_gain, ln2_bias).astype(jnp.bfloat16)
    rows_total = whole.shape[0]
    projected = jnp.dot(normed_one, qkv_full, preferred_element_type=jnp.float32) + b_qkv
    upward = jnp.dot(normed_two, up_full, preferred_element_type=jnp.float32)
    lengths_row = cache_lengths[0]
    query_owner, query_place = token_layout(lengths_row, rows_total)
    source = np.arange(rows_total).reshape(4, 4, 2, -1).transpose(2, 0, 1, 3).reshape(-1)
    query_owner = jnp.take(query_owner, source)
    query_place = jnp.take(query_place, source)
    queries = rotate(projected[:, :HD], query_place).astype(jnp.bfloat16)
    new_keys = rotate(projected[:, HD : 2 * HD], query_place).astype(jnp.bfloat16)
    new_values = projected[:, 2 * HD :].astype(jnp.bfloat16)
    hidden = jax.nn.gelu(upward + b_up, approximate=False).astype(jnp.bfloat16)
    slots = k_cache.shape[0]
    slot_owner, slot_place = slot_layout(lengths_row, slots)
    cache_scores = jnp.dot(queries, k_cache.T, preferred_element_type=jnp.float32) * scale
    cache_scores = jnp.where(
        visible(query_owner, query_place, slot_owner, slot_place), cache_scores, -jnp.inf
    )
    new_scores = jnp.dot(queries, new_keys.T, preferred_element_type=jnp.float32) * scale
    new_scores = jnp.where(
        visible(query_owner, query_place, query_owner, query_place), new_scores, -jnp.inf
    )
    top = jnp.maximum(jnp.max(cache_scores, axis=1), jnp.max(new_scores, axis=1))
    cache_weights = jnp.exp(cache_scores - top[:, None])
    new_weights = jnp.exp(new_scores - top[:, None])
    total = jnp.sum(cache_weights, axis=1) + jnp.sum(new_weights, axis=1)
    summed = jnp.dot(
        cache_weights.astype(jnp.bfloat16), v_cache, preferred_element_type=jnp.float32
    ) + jnp.dot(new_weights.astype(jnp.bfloat16), new_values, preferred_element_type=jnp.float32)
    attention = (summed / total[:, None]).astype(jnp.bfloat16)
    contract = (((1,), (1,)), ((), ()))
    mixed_in = jnp.concatenate([attention, hidden], axis=1)
    partial = lax.dot_general(mixed_in, second, contract, preferred_element_type=jnp.float32)
    partial = partial.reshape(rows_total, -1)
    heads = lax.axis_size("head")
    blocks = partial.reshape(2, heads // 2, tokens.shape[0], -1)
    core = lax.axis_index("head") % 2
    mine = lax.dynamic_index_in_dim(blocks, core, 0, keepdims=False)
    theirs = lax.dynamic_index_in_dim(blocks, 1 - core, 0, keepdims=False)
    swapped = lax.ppermute(
        theirs.astype(jnp.bfloat16), "head", [(index, index ^ 1) for index in range(heads)]
    )
    chip_sum = (mine + swapped.astype(jnp.float32)).astype(jnp.bfloat16)
    groups = [list(range(side, heads, 2)) for side in range(2)]
    exchanged = lax.all_to_all(chip_sum, "head", 0, 0, axis_index_groups=groups, tiled=True)
    partial_value = jnp.sum(exchanged.astype(jnp.float32), axis=0)
    mixed = tokens.astype(jnp.float32) + partial_value + b_dense + b_down
    return mixed.astype(jnp.bfloat16)


def solution(mesh):
    placed = (
        P(("tok", "head"), None),
        P(),
        P(),
        P(),
        P(),
        P("tok", "head"),
        P("head"),
        P("head", "tok"),
        P(),
        P("tok", "head"),
        P("head"),
        P("head", "tok"),
        P(),
        P("tok", "head"),
        P("tok", "head"),
        P("tok", None),
    )
    return jax.shard_map(
        body, mesh=mesh, in_specs=placed, out_specs=P(("tok", "head"), None), check_vma=False
    )
```

```python
import jax
import numpy as np
import jax.numpy as jnp
from jax import lax
from jax.sharding import PartitionSpec as P

HD = 128
ROT = 32
WINDOW = 2048
SINKS = 4


epsilon = 1e-05


def layer_norm(values, gain, shift):
    values = values.astype(jnp.float32)
    center = jnp.mean(values, axis=-1, keepdims=True)
    spread = jnp.mean(jnp.square(values - center), axis=-1, keepdims=True)
    return (values - center) * lax.rsqrt(spread + epsilon) * gain + shift


def rotate(values, positions):
    half = ROT // 2
    inverse = jnp.power(jnp.float32(10000.0), -jnp.arange(half, dtype=jnp.float32) * (2.0 / ROT))
    angles = (
        positions.astype(jnp.float32).reshape(positions.shape + (1,) * (values.ndim - 1)) * inverse
    )
    cosine = jnp.cos(angles)
    sine = jnp.sin(angles)
    first = values[..., :half]
    second = values[..., half:ROT]
    rest = values[..., ROT:]
    return jnp.concatenate(
        [first * cosine - second * sine, second * cosine + first * sine, rest], axis=-1
    )


def token_layout(lengths_row, group_rows):
    requests_count = lengths_row.shape[0]
    count_pre = group_rows - (requests_count - 1)
    index = jnp.arange(group_rows, dtype=jnp.int32)
    owner = jnp.maximum(index - (count_pre - 1), 0)
    table = owner[:, None] == jnp.arange(requests_count, dtype=jnp.int32)[None, :]
    start = jnp.sum(jnp.where(table, lengths_row[None, :], 0), axis=1)
    place = start + jnp.where(owner == 0, index, 0)
    return (owner, place)


def slot_layout(lengths_row, slots):
    starts = jnp.cumsum(lengths_row) - lengths_row
    index = jnp.arange(slots, dtype=jnp.int32)
    inside = index[:, None] >= starts[None, :]
    owner = jnp.sum(inside.astype(jnp.int32), axis=1) - 1
    begin = jnp.max(jnp.where(inside, starts[None, :], 0), axis=1)
    return (owner, index - begin)


def visible(query_owner, query_place, key_owner, key_place):
    same = query_owner[:, None] == key_owner[None, :]
    before = key_place[None, :] <= query_place[:, None]
    near = (key_place[None, :] < SINKS) | (query_place[:, None] - key_place[None, :] < WINDOW)
    return same & before & near


def stage_pairs(size, stride, shift, total):
    pairs = []
    for index in range(total):
        sub = (index // stride) % size
        pairs.append((index, index + ((sub + shift) % size - sub) * stride))
    return pairs


def gather_stage(stacked, size, stride):
    total = lax.axis_size("head")
    sub = (lax.axis_index("head") // stride) % size
    received = [stacked] + [
        lax.ppermute(stacked, "head", stage_pairs(size, stride, shift, total))
        for shift in range(1, size)
    ]
    return jnp.take(jnp.stack(received), (sub - jnp.arange(size)) % size, axis=0)


def head_gather(block):
    by_y = gather_stage(block, 4, 8)
    by_x = gather_stage(by_y, 4, 2)
    by_core = gather_stage(by_x, 2, 1)
    ordered = by_core.transpose((0, 2, 1) + tuple(range(3, by_core.ndim)))
    return ordered.reshape((-1,) + block.shape[1:])


def scatter_stage(chunks, size, stride):
    total = lax.axis_size("head")
    sub = (lax.axis_index("head") // stride) % size
    summed = lax.dynamic_index_in_dim(chunks, sub, 0, keepdims=False)
    for shift in range(1, size):
        outgoing = lax.dynamic_index_in_dim(chunks, (sub + shift) % size, 0, keepdims=False)
        summed = summed + lax.ppermute(
            outgoing.astype(jnp.bfloat16), "head", stage_pairs(size, stride, shift, total)
        ).astype(jnp.float32)
    return summed


def head_reduce_scatter(partial, rows):
    blocks = partial.reshape((4, 4, 2, rows) + partial.shape[1:])
    by_core = scatter_stage(jnp.moveaxis(blocks, 2, 0), 2, 1)
    by_x = scatter_stage(jnp.moveaxis(by_core, 1, 0), 4, 2)
    return scatter_stage(by_x, 4, 8)


def body(
    tokens,
    ln1_gain,
    ln1_bias,
    ln2_gain,
    ln2_bias,
    w_qkv,
    b_qkv,
    w_dense,
    b_dense,
    w_up,
    b_up,
    w_down,
    b_down,
    k_cache,
    v_cache,
    cache_lengths,
):
    scale = HD ** (-0.5)
    width_qkv = w_qkv.shape[1]
    width_up = w_up.shape[1]
    first = lax.all_gather(jnp.concatenate([w_qkv, w_up], axis=1), "tok", axis=0, tiled=False)
    second = lax.all_gather(
        jnp.concatenate([w_dense, w_down], axis=0), "tok", axis=0, tiled=False
    )
    parts = first.shape[0] * first.shape[1]
    qkv_full = first[:, :, :width_qkv].reshape(parts, width_qkv)
    up_full = first[:, :, width_qkv:].reshape(parts, width_up)
    whole = head_gather(tokens)
    normed_one = layer_norm(whole, ln1_gain, ln1_bias).astype(jnp.bfloat16)
    normed_two = layer_norm(whole, ln2_gain, ln2_bias).astype(jnp.bfloat16)
    rows_total = whole.shape[0]
    projected = jnp.dot(normed_one, qkv_full, preferred_element_type=jnp.float32) + b_qkv
    upward = jnp.dot(normed_two, up_full, preferred_element_type=jnp.float32)
    lengths_row = cache_lengths[0]
    query_owner, query_place = token_layout(lengths_row, rows_total)
    source = np.arange(rows_total).reshape(4, 4, 2, -1).transpose(2, 0, 1, 3).reshape(-1)
    query_owner = jnp.take(query_owner, source)
    query_place = jnp.take(query_place, source)
    queries = rotate(projected[:, :HD], query_place).astype(jnp.bfloat16)
    new_keys = rotate(projected[:, HD : 2 * HD], query_place).astype(jnp.bfloat16)
    new_values = projected[:, 2 * HD :].astype(jnp.bfloat16)
    hidden = jax.nn.gelu(upward + b_up, approximate=False).astype(jnp.bfloat16)
    slots = k_cache.shape[0]
    slot_owner, slot_place = slot_layout(lengths_row, slots)
    cache_scores = jnp.dot(queries, k_cache.T, preferred_element_type=jnp.float32) * scale
    cache_scores = jnp.where(
        visible(query_owner, query_place, slot_owner, slot_place), cache_scores, -jnp.inf
    )
    new_scores = jnp.dot(queries, new_keys.T, preferred_element_type=jnp.float32) * scale
    new_scores = jnp.where(
        visible(query_owner, query_place, query_owner, query_place), new_scores, -jnp.inf
    )
    top = jnp.maximum(jnp.max(cache_scores, axis=1), jnp.max(new_scores, axis=1))
    cache_weights = jnp.exp(cache_scores - top[:, None])
    new_weights = jnp.exp(new_scores - top[:, None])
    total = jnp.sum(cache_weights, axis=1) + jnp.sum(new_weights, axis=1)
    summed = jnp.dot(
        cache_weights.astype(jnp.bfloat16), v_cache, preferred_element_type=jnp.float32
    ) + jnp.dot(new_weights.astype(jnp.bfloat16), new_values, preferred_element_type=jnp.float32)
    attention = (summed / total[:, None]).astype(jnp.bfloat16)
    contract = (((1,), (1,)), ((), ()))
    mixed_in = jnp.concatenate([attention, hidden], axis=1)
    partial = lax.dot_general(mixed_in, second, contract, preferred_element_type=jnp.float32)
    partial = partial.reshape(rows_total, -1)
    heads = lax.axis_size("head")
    blocks = partial.astype(jnp.bfloat16).reshape(2, heads // 2, tokens.shape[0], -1)
    core = lax.axis_index("head") % 2
    mine = lax.dynamic_index_in_dim(blocks, core, 0, keepdims=False)
    theirs = lax.dynamic_index_in_dim(blocks, 1 - core, 0, keepdims=False)
    swapped = lax.ppermute(
        theirs, "head", [(index, index ^ 1) for index in range(heads)]
    )
    chip_sum = (mine.astype(jnp.float32) + swapped.astype(jnp.float32)).astype(jnp.bfloat16)
    groups = [list(range(side, heads, 2)) for side in range(2)]
    exchanged = lax.all_to_all(chip_sum, "head", 0, 0, axis_index_groups=groups, tiled=True)
    partial_value = jnp.sum(exchanged.astype(jnp.float32), axis=0)
    mixed = tokens.astype(jnp.float32) + partial_value + b_dense + b_down
    return mixed.astype(jnp.bfloat16)


def solution(mesh):
    placed = (
        P(("tok", "head"), None),
        P(),
        P(),
        P(),
        P(),
        P("tok", "head"),
        P("head"),
        P("head", "tok"),
        P(),
        P("tok", "head"),
        P("head"),
        P("head", "tok"),
        P(),
        P("tok", "head"),
        P("tok", "head"),
        P("tok", None),
    )
    return jax.shard_map(
        body, mesh=mesh, in_specs=placed, out_specs=P(("tok", "head"), None), check_vma=False
    )
```

```python
import jax
import numpy as np
import jax.numpy as jnp
from jax import lax
from jax.sharding import PartitionSpec as P

HD = 128
ROT = 32
WINDOW = 2048
SINKS = 4


epsilon = 1e-05


def layer_norm(values, gain, shift):
    values = values.astype(jnp.float32)
    center = jnp.mean(values, axis=-1, keepdims=True)
    spread = jnp.mean(jnp.square(values - center), axis=-1, keepdims=True)
    return (values - center) * lax.rsqrt(spread + epsilon) * gain + shift


def rotate(values, positions):
    half = ROT // 2
    inverse = jnp.power(jnp.float32(10000.0), -jnp.arange(half, dtype=jnp.float32) * (2.0 / ROT))
    angles = (
        positions.astype(jnp.float32).reshape(positions.shape + (1,) * (values.ndim - 1)) * inverse
    )
    cosine = jnp.cos(angles)
    sine = jnp.sin(angles)
    first = values[..., :half]
    second = values[..., half:ROT]
    rest = values[..., ROT:]
    return jnp.concatenate(
        [first * cosine - second * sine, second * cosine + first * sine, rest], axis=-1
    )


def token_layout(lengths_row, group_rows):
    requests_count = lengths_row.shape[0]
    count_pre = group_rows - (requests_count - 1)
    index = jnp.arange(group_rows, dtype=jnp.int32)
    owner = jnp.maximum(index - (count_pre - 1), 0)
    table = owner[:, None] == jnp.arange(requests_count, dtype=jnp.int32)[None, :]
    start = jnp.sum(jnp.where(table, lengths_row[None, :], 0), axis=1)
    place = start + jnp.where(owner == 0, index, 0)
    return (owner, place)


def slot_layout(lengths_row, slots):
    starts = jnp.cumsum(lengths_row) - lengths_row
    index = jnp.arange(slots, dtype=jnp.int32)
    inside = index[:, None] >= starts[None, :]
    owner = jnp.sum(inside.astype(jnp.int32), axis=1) - 1
    begin = jnp.max(jnp.where(inside, starts[None, :], 0), axis=1)
    return (owner, index - begin)


def visible(query_owner, query_place, key_owner, key_place):
    same = query_owner[:, None] == key_owner[None, :]
    before = key_place[None, :] <= query_place[:, None]
    near = (key_place[None, :] < SINKS) | (query_place[:, None] - key_place[None, :] < WINDOW)
    return same & before & near


def stage_pairs(size, stride, shift, total):
    pairs = []
    for index in range(total):
        sub = (index // stride) % size
        pairs.append((index, index + ((sub + shift) % size - sub) * stride))
    return pairs


def gather_stage(stacked, size, stride):
    total = lax.axis_size("head")
    sub = (lax.axis_index("head") // stride) % size
    received = [stacked] + [
        lax.ppermute(stacked, "head", stage_pairs(size, stride, shift, total))
        for shift in range(1, size)
    ]
    return jnp.take(jnp.stack(received), (sub - jnp.arange(size)) % size, axis=0)


def head_gather(block):
    by_y = gather_stage(block, 4, 8)
    by_x = gather_stage(by_y, 4, 2)
    by_core = gather_stage(by_x, 2, 1)
    ordered = by_core.transpose((0, 2, 1) + tuple(range(3, by_core.ndim)))
    return ordered.reshape((-1,) + block.shape[1:])


def scatter_stage(chunks, size, stride):
    total = lax.axis_size("head")
    sub = (lax.axis_index("head") // stride) % size
    summed = lax.dynamic_index_in_dim(chunks, sub, 0, keepdims=False)
    for shift in range(1, size):
        outgoing = lax.dynamic_index_in_dim(chunks, (sub + shift) % size, 0, keepdims=False)
        summed = summed + lax.ppermute(
            outgoing.astype(jnp.bfloat16), "head", stage_pairs(size, stride, shift, total)
        ).astype(jnp.float32)
    return summed


def head_reduce_scatter(partial, rows):
    blocks = partial.reshape((4, 4, 2, rows) + partial.shape[1:])
    by_core = scatter_stage(jnp.moveaxis(blocks, 2, 0), 2, 1)
    by_x = scatter_stage(jnp.moveaxis(by_core, 1, 0), 4, 2)
    return scatter_stage(by_x, 4, 8)


def body(
    tokens,
    ln1_gain,
    ln1_bias,
    ln2_gain,
    ln2_bias,
    w_qkv,
    b_qkv,
    w_dense,
    b_dense,
    w_up,
    b_up,
    w_down,
    b_down,
    k_cache,
    v_cache,
    cache_lengths,
):
    scale = HD ** (-0.5)
    width_qkv = w_qkv.shape[1]
    width_up = w_up.shape[1]
    first = lax.all_gather(jnp.concatenate([w_qkv, w_up], axis=1), "tok", axis=0, tiled=False)
    second = lax.all_gather(
        jnp.concatenate([w_dense, w_down], axis=0), "tok", axis=0, tiled=False
    )
    parts = first.shape[0] * first.shape[1]
    qkv_full = first[:, :, :width_qkv].reshape(parts, width_qkv)
    up_full = first[:, :, width_qkv:].reshape(parts, width_up)
    whole = head_gather(tokens)
    normed_one = layer_norm(whole, ln1_gain, ln1_bias).astype(jnp.bfloat16)
    normed_two = layer_norm(whole, ln2_gain, ln2_bias).astype(jnp.bfloat16)
    rows_total = whole.shape[0]
    projected = jnp.dot(normed_one, qkv_full, preferred_element_type=jnp.float32) + b_qkv
    upward = jnp.dot(normed_two, up_full, preferred_element_type=jnp.float32)
    lengths_row = cache_lengths[0]
    query_owner, query_place = token_layout(lengths_row, rows_total)
    source = np.arange(rows_total).reshape(4, 4, 2, -1).transpose(2, 0, 1, 3).reshape(-1)
    query_owner = jnp.take(query_owner, source)
    query_place = jnp.take(query_place, source)
    queries = rotate(projected[:, :HD], query_place).astype(jnp.bfloat16)
    new_keys = rotate(projected[:, HD : 2 * HD], query_place).astype(jnp.bfloat16)
    new_values = projected[:, 2 * HD :].astype(jnp.bfloat16)
    hidden = jax.nn.gelu(upward + b_up, approximate=False).astype(jnp.bfloat16)
    slots = k_cache.shape[0]
    slot_owner, slot_place = slot_layout(lengths_row, slots)
    cache_scores = jnp.dot(queries, k_cache.T, preferred_element_type=jnp.float32) * scale
    cache_scores = jnp.where(
        visible(query_owner, query_place, slot_owner, slot_place), cache_scores, -jnp.inf
    )
    new_scores = jnp.dot(queries, new_keys.T, preferred_element_type=jnp.float32) * scale
    new_scores = jnp.where(
        visible(query_owner, query_place, query_owner, query_place), new_scores, -jnp.inf
    )
    top = jnp.maximum(jnp.max(cache_scores, axis=1), jnp.max(new_scores, axis=1))
    cache_weights = jnp.exp(cache_scores - top[:, None])
    new_weights = jnp.exp(new_scores - top[:, None])
    total = jnp.sum(cache_weights, axis=1) + jnp.sum(new_weights, axis=1)
    summed = jnp.dot(
        cache_weights.astype(jnp.bfloat16), v_cache, preferred_element_type=jnp.float32
    ) + jnp.dot(new_weights.astype(jnp.bfloat16), new_values, preferred_element_type=jnp.float32)
    attention = (summed / total[:, None]).astype(jnp.bfloat16)
    contract = (((1,), (1,)), ((), ()))
    mixed_in = jnp.concatenate([attention, hidden], axis=1)
    heads = lax.axis_size("head")
    core = lax.axis_index("head") % 2
    groups = [list(range(side, heads, 2)) for side in range(2)]
    split = second.shape[0] // 2
    halves = []
    for pieces in (second[:split], second[split:]):
        partial = lax.dot_general(mixed_in, pieces, contract, preferred_element_type=jnp.float32)
        blocks = partial.astype(jnp.bfloat16).reshape(2, heads // 2, tokens.shape[0], -1)
        mine = lax.dynamic_index_in_dim(blocks, core, 0, keepdims=False)
        theirs = lax.dynamic_index_in_dim(blocks, 1 - core, 0, keepdims=False)
        swapped = lax.ppermute(theirs, "head", [(index, index ^ 1) for index in range(heads)])
        chip_sum = (mine.astype(jnp.float32) + swapped.astype(jnp.float32)).astype(jnp.bfloat16)
        exchanged = lax.all_to_all(chip_sum, "head", 0, 0, axis_index_groups=groups, tiled=True)
        halves.append(jnp.sum(exchanged.astype(jnp.float32), axis=0))
    partial_value = jnp.concatenate(halves, axis=1)
    mixed = tokens.astype(jnp.float32) + partial_value + b_dense + b_down
    return mixed.astype(jnp.bfloat16)


def solution(mesh):
    placed = (
        P(("tok", "head"), None),
        P(),
        P(),
        P(),
        P(),
        P("tok", "head"),
        P("head"),
        P("head", "tok"),
        P(),
        P("tok", "head"),
        P("head"),
        P("head", "tok"),
        P(),
        P("tok", "head"),
        P("tok", "head"),
        P("tok", None),
    )
    return jax.shard_map(
        body, mesh=mesh, in_specs=placed, out_specs=P(("tok", "head"), None), check_vma=False
    )
```

```python
import jax
import numpy as np
import jax.numpy as jnp
from jax import lax
from jax.sharding import PartitionSpec as P

HD = 128
ROT = 32
WINDOW = 2048
SINKS = 4


epsilon = 1e-05


def layer_norm(values, gain, shift):
    values = values.astype(jnp.float32)
    center = jnp.mean(values, axis=-1, keepdims=True)
    spread = jnp.mean(jnp.square(values - center), axis=-1, keepdims=True)
    return (values - center) * lax.rsqrt(spread + epsilon) * gain + shift


def rotate(values, positions):
    half = ROT // 2
    inverse = jnp.power(jnp.float32(10000.0), -jnp.arange(half, dtype=jnp.float32) * (2.0 / ROT))
    angles = (
        positions.astype(jnp.float32).reshape(positions.shape + (1,) * (values.ndim - 1)) * inverse
    )
    cosine = jnp.cos(angles)
    sine = jnp.sin(angles)
    first = values[..., :half]
    second = values[..., half:ROT]
    rest = values[..., ROT:]
    return jnp.concatenate(
        [first * cosine - second * sine, second * cosine + first * sine, rest], axis=-1
    )


def token_layout(lengths_row, group_rows):
    requests_count = lengths_row.shape[0]
    count_pre = group_rows - (requests_count - 1)
    index = jnp.arange(group_rows, dtype=jnp.int32)
    owner = jnp.maximum(index - (count_pre - 1), 0)
    table = owner[:, None] == jnp.arange(requests_count, dtype=jnp.int32)[None, :]
    start = jnp.sum(jnp.where(table, lengths_row[None, :], 0), axis=1)
    place = start + jnp.where(owner == 0, index, 0)
    return (owner, place)


def slot_layout(lengths_row, slots):
    starts = jnp.cumsum(lengths_row) - lengths_row
    index = jnp.arange(slots, dtype=jnp.int32)
    inside = index[:, None] >= starts[None, :]
    owner = jnp.sum(inside.astype(jnp.int32), axis=1) - 1
    begin = jnp.max(jnp.where(inside, starts[None, :], 0), axis=1)
    return (owner, index - begin)


def visible(query_owner, query_place, key_owner, key_place):
    same = query_owner[:, None] == key_owner[None, :]
    before = key_place[None, :] <= query_place[:, None]
    near = (key_place[None, :] < SINKS) | (query_place[:, None] - key_place[None, :] < WINDOW)
    return same & before & near


def stage_pairs(size, stride, shift, total):
    pairs = []
    for index in range(total):
        sub = (index // stride) % size
        pairs.append((index, index + ((sub + shift) % size - sub) * stride))
    return pairs


def gather_stage(stacked, size, stride):
    total = lax.axis_size("head")
    sub = (lax.axis_index("head") // stride) % size
    received = [stacked] + [
        lax.ppermute(stacked, "head", stage_pairs(size, stride, shift, total))
        for shift in range(1, size)
    ]
    return jnp.take(jnp.stack(received), (sub - jnp.arange(size)) % size, axis=0)


def head_gather(block):
    by_y = gather_stage(block, 4, 8)
    by_x = gather_stage(by_y, 4, 2)
    by_core = gather_stage(by_x, 2, 1)
    ordered = by_core.transpose((0, 2, 1) + tuple(range(3, by_core.ndim)))
    return ordered.reshape((-1,) + block.shape[1:])


def scatter_stage(chunks, size, stride):
    total = lax.axis_size("head")
    sub = (lax.axis_index("head") // stride) % size
    summed = lax.dynamic_index_in_dim(chunks, sub, 0, keepdims=False)
    for shift in range(1, size):
        outgoing = lax.dynamic_index_in_dim(chunks, (sub + shift) % size, 0, keepdims=False)
        summed = summed + lax.ppermute(
            outgoing.astype(jnp.bfloat16), "head", stage_pairs(size, stride, shift, total)
        ).astype(jnp.float32)
    return summed


def head_reduce_scatter(partial, rows):
    blocks = partial.reshape((4, 4, 2, rows) + partial.shape[1:])
    by_core = scatter_stage(jnp.moveaxis(blocks, 2, 0), 2, 1)
    by_x = scatter_stage(jnp.moveaxis(by_core, 1, 0), 4, 2)
    return scatter_stage(by_x, 4, 8)


def body(
    tokens,
    ln1_gain,
    ln1_bias,
    ln2_gain,
    ln2_bias,
    w_qkv,
    b_qkv,
    w_dense,
    b_dense,
    w_up,
    b_up,
    w_down,
    b_down,
    k_cache,
    v_cache,
    cache_lengths,
):
    scale = HD ** (-0.5)
    width_qkv = w_qkv.shape[1]
    width_up = w_up.shape[1]
    first = lax.all_gather(jnp.concatenate([w_qkv, w_up], axis=1), "tok", axis=0, tiled=False)
    second = lax.all_gather(
        jnp.concatenate([w_dense, w_down], axis=0), "tok", axis=0, tiled=False
    )
    parts = first.shape[0] * first.shape[1]
    qkv_full = first[:, :, :width_qkv].reshape(parts, width_qkv)
    up_full = first[:, :, width_qkv:].reshape(parts, width_up)
    whole = head_gather(tokens)
    normed_one = layer_norm(whole, ln1_gain, ln1_bias).astype(jnp.bfloat16)
    normed_two = layer_norm(whole, ln2_gain, ln2_bias).astype(jnp.bfloat16)
    rows_total = whole.shape[0]
    projected = jnp.dot(normed_one, qkv_full, preferred_element_type=jnp.float32) + b_qkv
    upward = jnp.dot(normed_two, up_full, preferred_element_type=jnp.float32)
    lengths_row = cache_lengths[0]
    query_owner, query_place = token_layout(lengths_row, rows_total)
    source = np.arange(rows_total).reshape(4, 4, 2, -1).transpose(2, 0, 1, 3).reshape(-1)
    query_owner = jnp.take(query_owner, source)
    query_place = jnp.take(query_place, source)
    queries = rotate(projected[:, :HD], query_place).astype(jnp.bfloat16)
    new_keys = rotate(projected[:, HD : 2 * HD], query_place).astype(jnp.bfloat16)
    new_values = projected[:, 2 * HD :].astype(jnp.bfloat16)
    hidden = jax.nn.gelu(upward + b_up, approximate=False).astype(jnp.bfloat16)
    slots = k_cache.shape[0]
    slot_owner, slot_place = slot_layout(lengths_row, slots)
    cache_scores = jnp.dot(queries, k_cache.T, preferred_element_type=jnp.float32) * scale
    cache_scores = jnp.where(
        visible(query_owner, query_place, slot_owner, slot_place), cache_scores, -jnp.inf
    )
    new_scores = jnp.dot(queries, new_keys.T, preferred_element_type=jnp.float32) * scale
    new_scores = jnp.where(
        visible(query_owner, query_place, query_owner, query_place), new_scores, -jnp.inf
    )
    top = jnp.maximum(jnp.max(cache_scores, axis=1), jnp.max(new_scores, axis=1))
    cache_weights = jnp.exp(cache_scores - top[:, None])
    new_weights = jnp.exp(new_scores - top[:, None])
    total = jnp.sum(cache_weights, axis=1) + jnp.sum(new_weights, axis=1)
    summed = jnp.dot(
        cache_weights.astype(jnp.bfloat16), v_cache, preferred_element_type=jnp.float32
    ) + jnp.dot(new_weights.astype(jnp.bfloat16), new_values, preferred_element_type=jnp.float32)
    attention = (summed / total[:, None]).astype(jnp.bfloat16)
    contract = (((1,), (1,)), ((), ()))
    mixed_in = jnp.concatenate([attention, hidden], axis=1)
    heads = lax.axis_size("head")
    core = lax.axis_index("head") % 2
    share = mixed_in.shape[0] // 2

    def output_rows(side):
        rows = lax.dynamic_slice_in_dim(mixed_in, side * share, share, 0)
        partial = lax.dot_general(rows, second, contract, preferred_element_type=jnp.float32)
        return partial.astype(jnp.bfloat16).reshape(heads // 2, tokens.shape[0], -1)

    swapped = lax.ppermute(
        output_rows(1 - core), "head", [(index, index ^ 1) for index in range(heads)]
    )
    mine = output_rows(core)
    chip_sum = (mine.astype(jnp.float32) + swapped.astype(jnp.float32)).astype(jnp.bfloat16)
    groups = [list(range(side, heads, 2)) for side in range(2)]
    exchanged = lax.all_to_all(chip_sum, "head", 0, 0, axis_index_groups=groups, tiled=True)
    partial_value = jnp.sum(exchanged.astype(jnp.float32), axis=0)
    mixed = tokens.astype(jnp.float32) + partial_value + b_dense + b_down
    return mixed.astype(jnp.bfloat16)


def solution(mesh):
    placed = (
        P(("tok", "head"), None),
        P(),
        P(),
        P(),
        P(),
        P("tok", "head"),
        P("head"),
        P("head", "tok"),
        P(),
        P("tok", "head"),
        P("head"),
        P("head", "tok"),
        P(),
        P("tok", "head"),
        P("tok", "head"),
        P("tok", None),
    )
    return jax.shard_map(
        body, mesh=mesh, in_specs=placed, out_specs=P(("tok", "head"), None), check_vma=False
    )
```

```python
import jax
import numpy as np
import jax.numpy as jnp
from jax import lax
from jax.sharding import PartitionSpec as P

HD = 128
ROT = 32
WINDOW = 2048
SINKS = 4


epsilon = 1e-05


def layer_norm(values, gain, shift):
    values = values.astype(jnp.float32)
    center = jnp.mean(values, axis=-1, keepdims=True)
    spread = jnp.mean(jnp.square(values - center), axis=-1, keepdims=True)
    return (values - center) * lax.rsqrt(spread + epsilon) * gain + shift


def rotate(values, positions):
    half = ROT // 2
    inverse = jnp.power(jnp.float32(10000.0), -jnp.arange(half, dtype=jnp.float32) * (2.0 / ROT))
    angles = (
        positions.astype(jnp.float32).reshape(positions.shape + (1,) * (values.ndim - 1)) * inverse
    )
    cosine = jnp.cos(angles)
    sine = jnp.sin(angles)
    first = values[..., :half]
    second = values[..., half:ROT]
    rest = values[..., ROT:]
    return jnp.concatenate(
        [first * cosine - second * sine, second * cosine + first * sine, rest], axis=-1
    )


def token_layout(lengths_row, group_rows):
    requests_count = lengths_row.shape[0]
    count_pre = group_rows - (requests_count - 1)
    index = jnp.arange(group_rows, dtype=jnp.int32)
    owner = jnp.maximum(index - (count_pre - 1), 0)
    table = owner[:, None] == jnp.arange(requests_count, dtype=jnp.int32)[None, :]
    start = jnp.sum(jnp.where(table, lengths_row[None, :], 0), axis=1)
    place = start + jnp.where(owner == 0, index, 0)
    return (owner, place)


def slot_layout(lengths_row, slots):
    starts = jnp.cumsum(lengths_row) - lengths_row
    index = jnp.arange(slots, dtype=jnp.int32)
    inside = index[:, None] >= starts[None, :]
    owner = jnp.sum(inside.astype(jnp.int32), axis=1) - 1
    begin = jnp.max(jnp.where(inside, starts[None, :], 0), axis=1)
    return (owner, index - begin)


def visible(query_owner, query_place, key_owner, key_place):
    same = query_owner[:, None] == key_owner[None, :]
    before = key_place[None, :] <= query_place[:, None]
    near = (key_place[None, :] < SINKS) | (query_place[:, None] - key_place[None, :] < WINDOW)
    return same & before & near


def stage_pairs(size, stride, shift, total):
    pairs = []
    for index in range(total):
        sub = (index // stride) % size
        pairs.append((index, index + ((sub + shift) % size - sub) * stride))
    return pairs


def gather_stage(stacked, size, stride):
    total = lax.axis_size("head")
    sub = (lax.axis_index("head") // stride) % size
    received = [stacked] + [
        lax.ppermute(stacked, "head", stage_pairs(size, stride, shift, total))
        for shift in range(1, size)
    ]
    return jnp.take(jnp.stack(received), (sub - jnp.arange(size)) % size, axis=0)


def head_gather(block):
    by_y = gather_stage(block, 4, 8)
    by_x = gather_stage(by_y, 4, 2)
    partner = lax.ppermute(by_x, "head", stage_pairs(2, 1, 1, lax.axis_size("head")))
    by_core = jnp.stack([by_x, partner])
    ordered = by_core.transpose((0, 2, 1) + tuple(range(3, by_core.ndim)))
    return ordered.reshape((-1,) + block.shape[1:])


def scatter_stage(chunks, size, stride):
    total = lax.axis_size("head")
    sub = (lax.axis_index("head") // stride) % size
    summed = lax.dynamic_index_in_dim(chunks, sub, 0, keepdims=False)
    for shift in range(1, size):
        outgoing = lax.dynamic_index_in_dim(chunks, (sub + shift) % size, 0, keepdims=False)
        summed = summed + lax.ppermute(
            outgoing.astype(jnp.bfloat16), "head", stage_pairs(size, stride, shift, total)
        ).astype(jnp.float32)
    return summed


def head_reduce_scatter(partial, rows):
    blocks = partial.reshape((4, 4, 2, rows) + partial.shape[1:])
    by_core = scatter_stage(jnp.moveaxis(blocks, 2, 0), 2, 1)
    by_x = scatter_stage(jnp.moveaxis(by_core, 1, 0), 4, 2)
    return scatter_stage(by_x, 4, 8)


def body(
    tokens,
    ln1_gain,
    ln1_bias,
    ln2_gain,
    ln2_bias,
    w_qkv,
    b_qkv,
    w_dense,
    b_dense,
    w_up,
    b_up,
    w_down,
    b_down,
    k_cache,
    v_cache,
    cache_lengths,
):
    scale = HD ** (-0.5)
    width_qkv = w_qkv.shape[1]
    width_up = w_up.shape[1]
    first = lax.all_gather(jnp.concatenate([w_qkv, w_up], axis=1), "tok", axis=0, tiled=False)
    second = lax.all_gather(
        jnp.concatenate([w_dense, w_down], axis=0), "tok", axis=0, tiled=False
    )
    parts = first.shape[0] * first.shape[1]
    qkv_full = first[:, :, :width_qkv].reshape(parts, width_qkv)
    up_full = first[:, :, width_qkv:].reshape(parts, width_up)
    whole = head_gather(tokens)
    normed_one = layer_norm(whole, ln1_gain, ln1_bias).astype(jnp.bfloat16)
    normed_two = layer_norm(whole, ln2_gain, ln2_bias).astype(jnp.bfloat16)
    rows_total = whole.shape[0]
    projected = jnp.dot(normed_one, qkv_full, preferred_element_type=jnp.float32) + b_qkv
    upward = jnp.dot(normed_two, up_full, preferred_element_type=jnp.float32)
    lengths_row = cache_lengths[0]
    query_owner, query_place = token_layout(lengths_row, rows_total)
    source = np.arange(rows_total).reshape(4, 4, 2, -1).transpose(2, 0, 1, 3)
    core = lax.axis_index("head") % 2
    source = jnp.where(core == 0, source.reshape(-1), source[::-1].reshape(-1))
    query_owner = jnp.take(query_owner, source)
    query_place = jnp.take(query_place, source)
    queries = rotate(projected[:, :HD], query_place).astype(jnp.bfloat16)
    new_keys = rotate(projected[:, HD : 2 * HD], query_place).astype(jnp.bfloat16)
    new_values = projected[:, 2 * HD :].astype(jnp.bfloat16)
    hidden = jax.nn.gelu(upward + b_up, approximate=False).astype(jnp.bfloat16)
    slots = k_cache.shape[0]
    slot_owner, slot_place = slot_layout(lengths_row, slots)
    cache_scores = jnp.dot(queries, k_cache.T, preferred_element_type=jnp.float32) * scale
    cache_scores = jnp.where(
        visible(query_owner, query_place, slot_owner, slot_place), cache_scores, -jnp.inf
    )
    new_scores = jnp.dot(queries, new_keys.T, preferred_element_type=jnp.float32) * scale
    new_scores = jnp.where(
        visible(query_owner, query_place, query_owner, query_place), new_scores, -jnp.inf
    )
    top = jnp.maximum(jnp.max(cache_scores, axis=1), jnp.max(new_scores, axis=1))
    cache_weights = jnp.exp(cache_scores - top[:, None])
    new_weights = jnp.exp(new_scores - top[:, None])
    total = jnp.sum(cache_weights, axis=1) + jnp.sum(new_weights, axis=1)
    summed = jnp.dot(
        cache_weights.astype(jnp.bfloat16), v_cache, preferred_element_type=jnp.float32
    ) + jnp.dot(new_weights.astype(jnp.bfloat16), new_values, preferred_element_type=jnp.float32)
    attention = (summed / total[:, None]).astype(jnp.bfloat16)
    contract = (((1,), (1,)), ((), ()))
    mixed_in = jnp.concatenate([attention, hidden], axis=1)
    partial = lax.dot_general(mixed_in, second, contract, preferred_element_type=jnp.float32)
    partial = partial.reshape(rows_total, -1)
    heads = lax.axis_size("head")
    blocks = partial.astype(jnp.bfloat16).reshape(2, heads // 2, tokens.shape[0], -1)
    mine = blocks[0]
    theirs = blocks[1]
    swapped = lax.ppermute(
        theirs, "head", [(index, index ^ 1) for index in range(heads)]
    )
    chip_sum = (mine.astype(jnp.float32) + swapped.astype(jnp.float32)).astype(jnp.bfloat16)
    groups = [list(range(side, heads, 2)) for side in range(2)]
    exchanged = lax.all_to_all(chip_sum, "head", 0, 0, axis_index_groups=groups, tiled=True)
    partial_value = jnp.sum(exchanged.astype(jnp.float32), axis=0)
    mixed = tokens.astype(jnp.float32) + partial_value + b_dense + b_down
    return mixed.astype(jnp.bfloat16)


def solution(mesh):
    placed = (
        P(("tok", "head"), None),
        P(),
        P(),
        P(),
        P(),
        P("tok", "head"),
        P("head"),
        P("head", "tok"),
        P(),
        P("tok", "head"),
        P("head"),
        P("head", "tok"),
        P(),
        P("tok", "head"),
        P("tok", "head"),
        P("tok", None),
    )
    return jax.shard_map(
        body, mesh=mesh, in_specs=placed, out_specs=P(("tok", "head"), None), check_vma=False
    )
```
